512 devices in a mesh: req: 64 (over y, z), tp: 8 (over x, core).
Axes of the slice: x: 4, y: 8, z: 8, core: 2. Of those that a mesh axis runs over, the one named last changes fastest.
Arguments:
- hidden_in: bfloat16 [64, 512, 1024], P(None, 'req', 'tp'), may hold values from -64 to 64
- cache_keys: bfloat16 [64, 512, 1024], P('req', None, 'tp'), may hold values from -250 to 250
- cache_values: bfloat16 [64, 512, 1024], P('req', None, 'tp'), may hold values from -6 to 6
- cache_lengths: int32 [64], replicated, may hold values from 32 to 512, as said below
- owner_order: int32 [64], replicated, may hold values from 0 to 63, as said below
- request_slot: int32 [64], replicated, may hold values from 0 to 63, as said below
- proj_weight: bfloat16 [3, 1024, 1024], P(None, None, 'tp'), may hold values from -0.0625 to 0.0625
- proj_bias: bfloat16 [3, 1024], P(None, 'tp'), may hold values from -1.5 to 1.5
- output_weight: bfloat16 [1024, 1024], P('tp'), may hold values from -0.75 to 0.75
- output_bias: bfloat16 [1024], replicated, may hold values from -2.5 to 2.5
- norm_gains: bfloat16 [2, 1024], replicated, may hold values from 0.5 to 1.5
- norm_biases: bfloat16 [2, 1024], replicated, may hold values from -2.5 to 2.5
- widen_weight: bfloat16 [1024, 4096], P(None, 'tp'), may hold values from -0.1875 to 0.1875
- widen_bias: bfloat16 [4096], P('tp'), may hold values from -2.5 to 2.5
- narrow_weight: bfloat16 [4096, 1024], P('tp'), may hold values from -0.09375 to 0.09375
- narrow_bias: bfloat16 [1024], replicated, may hold values from -2.5 to 2.5
Outputs:
- hidden_out: bfloat16 [64, 512, 1024], P(None, 'req', 'tp')
- new_cache: bfloat16 [2, 64, 512, 1024], P(None, 'req', None, 'tp')
The draws below stay inside these ranges and needn't reach their ends.
Inputs may be any that keep to these rules, and one draw needn't show every extreme that they name: owner_order is a permutation of the requests; owner slot s lies on index s // 1 of req. request_slot[owner_order[s]] = s for every slot s. `cache_lengths`: given in request order; the longest is exactly 512.
All inputs are finite; a program needn't handle non-finite values.
Results may differ from the reference program's by a relative error of at most 0.014.
Values may be sent and summed in bfloat16 or wider, within the bound.
No kernel may reach another device: no remote copies, remote signals or barrier semaphores. Data moves between devices by JAX's collectives and lax.ppermute only.
A program may use at most 64 MiB of HBM per device.

```python
import math
import jax
import jax.numpy as jnp
from jax import lax

D = 1024
HEADS = 16
HD = 64
FF = 4096
FRESH = 512
CACHE_MAX = 512
REQ = 64
N_TP = 8


def shuffled_requests(key):
    return jax.random.permutation(jax.random.fold_in(key, 11), REQ).astype(jnp.int32)


def draw_owner_order(key, part):
    return shuffled_requests(key)


def draw_request_slot(key, part):
    shuffled = shuffled_requests(key)
    return jnp.argsort(shuffled, stable=True).astype(jnp.int32)


def draw_cache_lengths(key, part):
    shortest = max(2, CACHE_MAX // 16)
    draw_one = jax.random.randint(jax.random.fold_in(key, 21), (REQ,), shortest, CACHE_MAX + 1)
    draw_two = jax.random.randint(jax.random.fold_in(key, 22), (REQ,), shortest, CACHE_MAX + 1)
    longest = jax.random.randint(jax.random.fold_in(key, 23), (), 0, REQ)
    lengths = jnp.minimum(draw_one, draw_two)
    lengths = jnp.where(jnp.arange(REQ) == longest, CACHE_MAX, lengths)
    return lengths.astype(jnp.int32)


def draw_hidden_in(key, part):
    column_key = jax.random.fold_in(key, 31)
    row_key = jax.random.fold_in(key, 32)
    base_key = jax.random.fold_in(key, 33)
    column_scale = jnp.exp(jax.random.uniform(column_key, (1, 1, D), jnp.float32, math.log(0.4), math.log(4.0)))
    row_scale = jnp.exp(jax.random.uniform(row_key, (REQ, FRESH, 1), jnp.float32, math.log(0.4), math.log(4.0)))
    base_draw = jnp.clip(jax.random.normal(base_key, (REQ, FRESH, D), jnp.float32), -4.0, 4.0)
    return (base_draw * column_scale * row_scale).astype(jnp.bfloat16)


def draw_cache_keys(key, part):
    base_key = jax.random.fold_in(key, 41)
    features = HEADS * HD
    stored_keys = jnp.clip(jax.random.normal(base_key, (REQ, CACHE_MAX, features), jnp.float32), -5.0, 5.0)
    return stored_keys.astype(jnp.bfloat16)


def steps_of(key, dims, split, low, largest):
    gain, own = 1.0, jax.random.fold_in(key, 6)
    for axis_at, parts in split:
        draws = jnp.exp(jax.random.uniform(jax.random.fold_in(own, axis_at), (parts,), jnp.float32, low / len(split), largest / len(split)))
        gain = gain * jnp.repeat(draws, dims[axis_at] // parts).reshape([-1 if axis == axis_at else 1 for axis in range(len(dims))])
    return gain


def gaussian(key, extent, width, bound, pieces=(), kind=jnp.bfloat16):
    entries = width * jax.random.normal(key, extent, jnp.float32)
    if pieces:
        entries = entries * steps_of(key, extent, pieces, -0.22, 0.18)
    return jnp.clip(entries, -bound, bound).astype(kind)


def setup_inputs(seed: int = 0) -> dict:
    arg_keys = jax.random.split(jax.random.key(seed), 17)
    hidden_in = draw_hidden_in(jax.random.fold_in(arg_keys[16], 71), 0)
    cache_keys = draw_cache_keys(jax.random.fold_in(arg_keys[16], 71), 0)
    cache_values = gaussian(arg_keys[2], (REQ, CACHE_MAX, HEADS * HD), 1.0, 6.0, ((0, 64), (2, 8)))
    cache_lengths = draw_cache_lengths(jax.random.fold_in(arg_keys[16], 71), 0)
    owner_order = draw_owner_order(jax.random.fold_in(arg_keys[16], 71), 0)
    request_slot = draw_request_slot(jax.random.fold_in(arg_keys[16], 71), 0)
    proj_weight = gaussian(arg_keys[6], (3, D, HEADS * HD), (8 * D) ** -0.5, 0.0625, ((2, 8),))
    proj_bias = gaussian(arg_keys[7], (3, HEADS * HD), 0.3, 1.5, ((1, 8),))
    output_weight = gaussian(arg_keys[8], (HEADS * HD, D), (HEADS * HD // 16) ** -0.5, 0.75, ((0, 8),))
    output_bias = gaussian(arg_keys[9], (D,), 0.5, 2.5)
    norm_gains = jnp.clip(1.0 + 0.1 * jax.random.normal(arg_keys[10], (2, D), jnp.float32), 0.5, 1.5).astype(jnp.bfloat16)
    norm_biases = gaussian(arg_keys[11], (2, D), 0.5, 2.5)
    widen_weight = gaussian(arg_keys[12], (D, FF), D ** -0.5, 0.1875, ((1, 8),))
    widen_bias = gaussian(arg_keys[13], (FF,), 0.5, 2.5, ((0, 8),))
    narrow_weight = gaussian(arg_keys[14], (FF, D), FF ** -0.5, 0.09375, ((0, 8),))
    narrow_bias = gaussian(arg_keys[15], (D,), 0.5, 2.5)
    return {"hidden_in": hidden_in, "cache_keys": cache_keys, "cache_values": cache_values, "cache_lengths": cache_lengths, "owner_order": owner_order, "request_slot": request_slot, "proj_weight": proj_weight, "proj_bias": proj_bias, "output_weight": output_weight, "output_bias": output_bias, "norm_gains": norm_gains, "norm_biases": norm_biases, "widen_weight": widen_weight, "widen_bias": widen_bias, "narrow_weight": narrow_weight, "narrow_bias": narrow_bias}


def layer_norm(values, scale_row, shift_row):
    average = lax.optimization_barrier(jnp.mean(values, axis=-1, keepdims=True))
    centred = values - average
    spread = lax.optimization_barrier(jnp.mean(centred * centred, axis=-1, keepdims=True))
    return centred * lax.rsqrt(spread + 1e-05) * scale_row.astype(jnp.float32) + shift_row.astype(jnp.float32)

def group_sum(left_side, right_side):
    group_width = left_side.shape[1] // N_TP
    group_total = jnp.zeros((left_side.shape[0], right_side.shape[1]), jnp.float32)
    for group_index in range(N_TP):
        low_edge = group_index * group_width
        partial_term = jnp.dot(left_side[:, low_edge:low_edge + group_width], right_side[low_edge:low_edge + group_width], preferred_element_type=jnp.float32)
        group_total = group_total + lax.optimization_barrier(partial_term.astype(jnp.bfloat16)).astype(jnp.float32)
    return group_total

def reference(hidden_in, cache_keys, cache_values, cache_lengths, owner_order, request_slot, proj_weight, proj_bias, output_weight, output_bias, norm_gains, norm_biases, widen_weight, widen_bias, narrow_weight, narrow_bias):
    routed = jnp.take(hidden_in, owner_order, axis=0)
    lengths = jnp.take(cache_lengths, owner_order)

    def per_slot(fields):
        token_rows, slot_keys, slot_values, length = fields
        projected = jnp.einsum('td,cdf->ctf', token_rows.astype(jnp.float32), proj_weight.astype(jnp.float32)) + proj_bias.astype(jnp.float32)[:, None, :]
        query_rows = (projected[0] * HD ** (-0.5)).astype(jnp.bfloat16)
        key_rows = projected[1].astype(jnp.bfloat16)
        value_rows = projected[2].astype(jnp.bfloat16)
        fresh_len = token_rows.shape[0]
        stored = slot_keys.shape[0]
        every_key = jnp.concatenate([slot_keys, key_rows], axis=0)
        every_value = jnp.concatenate([slot_values, value_rows], axis=0)
        cache_mask = jnp.broadcast_to(jnp.arange(stored)[None, :] < length, (fresh_len, stored))
        self_mask = jnp.arange(fresh_len)[:, None] >= jnp.arange(fresh_len)[None, :]
        allowed = jnp.concatenate([cache_mask, self_mask], axis=1)
        query_heads = query_rows.astype(jnp.float32).reshape(fresh_len, HEADS, HD)
        key_heads = every_key.astype(jnp.float32).reshape(stored + fresh_len, HEADS, HD)
        value_heads = every_value.astype(jnp.float32).reshape(stored + fresh_len, HEADS, HD)
        scores = jnp.einsum('thd,shd->hts', query_heads, key_heads)
        scores = jnp.where(allowed[None], scores, -jnp.inf)
        row_top = lax.optimization_barrier(jnp.max(scores, axis=2, keepdims=True))
        raised = jnp.exp(scores - row_top)
        total = lax.optimization_barrier(jnp.sum(raised, axis=2, keepdims=True))
        weights = raised.astype(jnp.bfloat16)
        context = jnp.einsum('hts,shd->thd', weights.astype(jnp.float32), value_heads)
        context = context / jnp.transpose(total, (1, 0, 2))
        context = context.reshape(fresh_len, HEADS * HD).astype(jnp.bfloat16)
        attended = group_sum(context, output_weight) + output_bias.astype(jnp.float32)
        normed = layer_norm(token_rows.astype(jnp.float32) + attended, norm_gains[0], norm_biases[0]).astype(jnp.bfloat16)
        widened = jnp.dot(normed, widen_weight, preferred_element_type=jnp.float32) + widen_bias.astype(jnp.float32)
        activated = jax.nn.gelu(widened, approximate=False).astype(jnp.bfloat16)
        fed_total = group_sum(activated, narrow_weight) + narrow_bias.astype(jnp.float32)
        updated = layer_norm(normed.astype(jnp.float32) + fed_total, norm_gains[1], norm_biases[1]).astype(jnp.bfloat16)
        return (updated, key_rows, value_rows)
    updated, key_rows, value_rows = lax.map(per_slot, (routed, cache_keys, cache_values, lengths))
    hidden_out = jnp.take(updated, request_slot, axis=0)
    new_cache = jnp.stack([key_rows, value_rows], axis=0)
    return (hidden_out, new_cache)
```

```python
import jax
import jax.numpy as jnp
from jax import lax
from jax.sharding import PartitionSpec as P

HD = 64


def layer_norm(values, scale_row, shift_row):
    average = jnp.mean(values, axis=-1, keepdims=True)
    centred = values - average
    spread = jnp.mean(centred * centred, axis=-1, keepdims=True)
    return centred * lax.rsqrt(spread + 1e-05) * scale_row.astype(jnp.float32) + shift_row.astype(
        jnp.float32
    )


def split_heads(rows_block):
    return rows_block.reshape(rows_block.shape[0], -1, HD)


def block_scores(query_heads, keys_block, allowed):
    scores = jnp.einsum(
        "thd,shd->hts", query_heads, split_heads(keys_block), preferred_element_type=jnp.float32
    )
    return jnp.where(allowed[None], scores, -jnp.inf)


def to_rows(factor):
    return jnp.transpose(factor, (1, 0, 2))


def slot_attention(query_rows, key_rows, value_rows, slot_keys, slot_values, length):
    fresh_len = query_rows.shape[0]
    block_len = min(512, slot_keys.shape[0])
    block_count = slot_keys.shape[0] // block_len
    query_heads = split_heads(query_rows)
    self_mask = jnp.arange(fresh_len)[:, None] >= jnp.arange(fresh_len)[None, :]
    self_scores = block_scores(query_heads, key_rows, self_mask)
    row_top = jnp.max(self_scores, axis=2, keepdims=True)
    raised = jnp.exp(self_scores - row_top)
    row_total = jnp.sum(raised, axis=2, keepdims=True)
    context = jnp.einsum(
        "hts,shd->thd",
        raised.astype(jnp.bfloat16),
        split_heads(value_rows),
        preferred_element_type=jnp.float32,
    )
    positions = jnp.arange(block_len)

    def one_block(number, carry):
        old_top, old_total, running = carry
        begin_at = number * block_len
        keys_block = lax.dynamic_slice_in_dim(slot_keys, begin_at, block_len)
        values_block = lax.dynamic_slice_in_dim(slot_values, begin_at, block_len)
        allowed = jnp.broadcast_to((begin_at + positions < length)[None, :], (fresh_len, block_len))
        scores = block_scores(query_heads, keys_block, allowed)
        new_top = jnp.maximum(old_top, jnp.max(scores, axis=2, keepdims=True))
        factor = jnp.exp(old_top - new_top)
        block_raised = jnp.exp(scores - new_top)
        new_total = old_total * factor + jnp.sum(block_raised, axis=2, keepdims=True)
        added = jnp.einsum(
            "hts,shd->thd",
            block_raised.astype(jnp.bfloat16),
            split_heads(values_block),
            preferred_element_type=jnp.float32,
        )
        return (new_top, new_total, running * to_rows(factor) + added)

    row_top, row_total, context = lax.fori_loop(
        0, block_count, one_block, (row_top, row_total, context)
    )
    context = context / to_rows(row_total)
    return context.reshape(fresh_len, -1).astype(jnp.bfloat16)


def gather_tp(block, tp_count, axis):
    copies = jnp.broadcast_to(
        jnp.expand_dims(block, axis), block.shape[:axis] + (tp_count,) + block.shape[axis:]
    )
    got = lax.all_to_all(copies, "tp", axis, axis, tiled=True)
    return got.reshape(block.shape[:axis] + (-1,) + block.shape[axis + 1 :])


def reduce_tp(partial, tp_count):
    rows = partial.shape[0] // tp_count
    got = lax.all_to_all(partial.reshape(tp_count, rows, -1), "tp", 0, 0, tiled=True)
    return jnp.sum(got.astype(jnp.float32), axis=0)


def on_device(
    hidden_in,
    cache_keys,
    cache_values,
    cache_lengths,
    owner_order,
    request_slot,
    proj_weight,
    proj_bias,
    output_weight,
    output_bias,
    norm_gains,
    norm_biases,
    widen_weight,
    widen_bias,
    narrow_weight,
    narrow_bias,
):
    tp_count = lax.axis_size("tp")
    tp_index = lax.axis_index("tp")
    slot_index = lax.axis_index("req")
    length = cache_lengths[owner_order[slot_index]]
    own_cols = lax.all_to_all(
        jnp.take(hidden_in, owner_order, axis=0), "req", split_axis=0, concat_axis=1, tiled=True
    )[0]
    fresh_len = own_cols.shape[0]
    width = own_cols.shape[1] * tp_count
    token_rows = gather_tp(own_cols, tp_count, 1)
    projected = (
        jnp.einsum("td,cdf->ctf", token_rows, proj_weight, preferred_element_type=jnp.float32)
        + proj_bias.astype(jnp.float32)[:, None, :]
    )
    query_rows = (projected[0] * HD ** (-0.5)).astype(jnp.bfloat16)
    key_rows = projected[1].astype(jnp.bfloat16)
    value_rows = projected[2].astype(jnp.bfloat16)
    new_cache = jnp.stack([key_rows, value_rows], axis=0)[:, None]
    context = slot_attention(
        query_rows, key_rows, value_rows, cache_keys[0], cache_values[0], length
    )
    rows = fresh_len // tp_count
    own_rows = lax.dynamic_slice_in_dim(token_rows, tp_index * rows, rows)
    attended = reduce_tp(
        jnp.dot(context, output_weight, preferred_element_type=jnp.float32).astype(jnp.bfloat16),
        tp_count,
    )
    normed = layer_norm(
        own_rows.astype(jnp.float32) + attended + output_bias.astype(jnp.float32),
        norm_gains[0],
        norm_biases[0],
    ).astype(jnp.bfloat16)
    normed_all = gather_tp(normed, tp_count, 0)
    widened = jnp.dot(normed_all, widen_weight, preferred_element_type=jnp.float32) + widen_bias.astype(
        jnp.float32
    )
    activated = jax.nn.gelu(widened, approximate=False).astype(jnp.bfloat16)
    fed_total = reduce_tp(
        jnp.dot(activated, narrow_weight, preferred_element_type=jnp.float32).astype(jnp.bfloat16),
        tp_count,
    )
    updated = layer_norm(
        normed.astype(jnp.float32) + fed_total + narrow_bias.astype(jnp.float32),
        norm_gains[1],
        norm_biases[1],
    ).astype(jnp.bfloat16)
    by_cols = lax.all_to_all(
        updated.reshape(rows, tp_count, width // tp_count), "tp", 1, 0, tiled=True
    ).reshape(fresh_len, width // tp_count)
    returned = lax.all_to_all(by_cols[None], "req", split_axis=1, concat_axis=0, tiled=True)
    hidden_out = jnp.take(returned, request_slot, axis=0)
    return (hidden_out, new_cache)


def solution(mesh):
    in_specs = (
        P(None, "req", "tp"),
        P("req", None, "tp"),
        P("req", None, "tp"),
        P(),
        P(),
        P(),
        P(None, None, "tp"),
        P(None, "tp"),
        P("tp", None),
        P(),
        P(),
        P(),
        P(None, "tp"),
        P("tp"),
        P("tp", None),
        P(),
    )
    out_specs = (P(None, "req", "tp"), P(None, "req", None, "tp"))
    return jax.shard_map(
        on_device, mesh=mesh, in_specs=in_specs, out_specs=out_specs, check_vma=False
    )
```

```python
import jax
import jax.numpy as jnp
from jax import lax
from jax.sharding import PartitionSpec as P

HD = 64


def layer_norm(values, scale_row, shift_row):
    average = jnp.mean(values, axis=-1, keepdims=True)
    centred = values - average
    spread = jnp.mean(centred * centred, axis=-1, keepdims=True)
    return centred * lax.rsqrt(spread + 1e-05) * scale_row.astype(jnp.float32) + shift_row.astype(
        jnp.float32
    )


def split_heads(rows_block):
    return rows_block.reshape(rows_block.shape[0], -1, HD)


def block_scores(query_heads, keys_block, allowed):
    scores = jnp.einsum(
        "thd,shd->hts", query_heads, split_heads(keys_block), preferred_element_type=jnp.float32
    )
    return jnp.where(allowed[None], scores, -jnp.inf)


def to_rows(factor):
    return jnp.transpose(factor, (1, 0, 2))


def slot_attention(query_rows, key_rows, value_rows, slot_keys, slot_values, length):
    fresh_len = query_rows.shape[0]
    block_len = min(512, slot_keys.shape[0])
    block_count = slot_keys.shape[0] // block_len
    query_heads = split_heads(query_rows)
    self_mask = jnp.arange(fresh_len)[:, None] >= jnp.arange(fresh_len)[None, :]
    self_scores = block_scores(query_heads, key_rows, self_mask)
    row_top = jnp.max(self_scores, axis=2, keepdims=True)
    raised = jnp.exp(self_scores - row_top)
    row_total = jnp.sum(raised, axis=2, keepdims=True)
    context = jnp.einsum(
        "hts,shd->thd",
        raised.astype(jnp.bfloat16),
        split_heads(value_rows),
        preferred_element_type=jnp.float32,
    )
    positions = jnp.arange(block_len)

    def one_block(number, carry):
        old_top, old_total, running = carry
        begin_at = number * block_len
        keys_block = lax.dynamic_slice_in_dim(slot_keys, begin_at, block_len)
        values_block = lax.dynamic_slice_in_dim(slot_values, begin_at, block_len)
        allowed = jnp.broadcast_to((begin_at + positions < length)[None, :], (fresh_len, block_len))
        scores = block_scores(query_heads, keys_block, allowed)
        new_top = jnp.maximum(old_top, jnp.max(scores, axis=2, keepdims=True))
        factor = jnp.exp(old_top - new_top)
        block_raised = jnp.exp(scores - new_top)
        new_total = old_total * factor + jnp.sum(block_raised, axis=2, keepdims=True)
        added = jnp.einsum(
            "hts,shd->thd",
            block_raised.astype(jnp.bfloat16),
            split_heads(values_block),
            preferred_element_type=jnp.float32,
        )
        return (new_top, new_total, running * to_rows(factor) + added)

    row_top, row_total, context = lax.fori_loop(
        0, block_count, one_block, (row_top, row_total, context)
    )
    context = context / to_rows(row_total)
    return context.reshape(fresh_len, -1).astype(jnp.bfloat16)


def gather_tp(block, tp_count, axis):
    copies = jnp.broadcast_to(
        jnp.expand_dims(block, axis), block.shape[:axis] + (tp_count,) + block.shape[axis:]
    )
    got = lax.all_to_all(copies, "tp", axis, axis, tiled=True)
    return got.reshape(block.shape[:axis] + (-1,) + block.shape[axis + 1 :])


def reduce_tp(partial, tp_count):
    rows = partial.shape[0] // tp_count
    got = lax.all_to_all(partial.reshape(tp_count, rows, -1), "tp", 0, 0, tiled=True)
    return jnp.sum(got.astype(jnp.float32), axis=0)


def on_device(
    hidden_in,
    cache_keys,
    cache_values,
    cache_lengths,
    owner_order,
    request_slot,
    proj_weight,
    proj_bias,
    output_weight,
    output_bias,
    norm_gains,
    norm_biases,
    widen_weight,
    widen_bias,
    narrow_weight,
    narrow_bias,
):
    tp_count = lax.axis_size("tp")
    tp_index = lax.axis_index("tp")
    slot_index = lax.axis_index("req")
    length = cache_lengths[owner_order[slot_index]]
    own_cols = lax.all_to_all(
        hidden_in.at[owner_order].get(mode="promise_in_bounds", unique_indices=True),
        "req",
        split_axis=0,
        concat_axis=1,
        tiled=True,
    )[0]
    fresh_len = own_cols.shape[0]
    width = own_cols.shape[1] * tp_count
    token_rows = gather_tp(own_cols, tp_count, 1)
    projected = [
        jnp.dot(token_rows, proj_weight[c], preferred_element_type=jnp.float32)
        + proj_bias[c].astype(jnp.float32)
        for c in range(3)
    ]
    query_rows = (projected[0] * HD ** (-0.5)).astype(jnp.bfloat16)
    key_rows = projected[1].astype(jnp.bfloat16)
    value_rows = projected[2].astype(jnp.bfloat16)
    new_cache = jnp.stack([key_rows, value_rows], axis=0)[:, None]
    context = slot_attention(
        query_rows, key_rows, value_rows, cache_keys[0], cache_values[0], length
    )
    rows = fresh_len // tp_count
    own_rows = lax.optimization_barrier(
        lax.dynamic_slice_in_dim(token_rows, tp_index * rows, rows).astype(jnp.float32)
        + output_bias.astype(jnp.float32)
    )
    attended = reduce_tp(
        jnp.dot(context, output_weight, preferred_element_type=jnp.float32).astype(jnp.bfloat16),
        tp_count,
    )
    normed = layer_norm(
        own_rows + attended,
        norm_gains[0],
        norm_biases[0],
    ).astype(jnp.bfloat16)
    normed_all = gather_tp(normed, tp_count, 0)
    widened = jnp.dot(normed_all, widen_weight, preferred_element_type=jnp.float32) + widen_bias.astype(
        jnp.float32
    )
    activated = lax.optimization_barrier(
        jax.nn.gelu(widened, approximate=False).astype(jnp.bfloat16)
    )
    fed_total = reduce_tp(
        jnp.dot(activated, narrow_weight, preferred_element_type=jnp.float32).astype(jnp.bfloat16),
        tp_count,
    )
    updated = layer_norm(
        normed.astype(jnp.float32) + fed_total + narrow_bias.astype(jnp.float32),
        norm_gains[1],
        norm_biases[1],
    ).astype(jnp.bfloat16)
    by_cols = lax.all_to_all(
        updated.reshape(rows, tp_count, width // tp_count), "tp", 1, 0, tiled=True
    ).reshape(fresh_len, width // tp_count)
    returned = lax.all_to_all(by_cols[None], "req", split_axis=1, concat_axis=0, tiled=True)
    hidden_out = returned.at[request_slot].get(mode="promise_in_bounds", unique_indices=True)
    return (hidden_out, new_cache)


def solution(mesh):
    in_specs = (
        P(None, "req", "tp"),
        P("req", None, "tp"),
        P("req", None, "tp"),
        P(),
        P(),
        P(),
        P(None, None, "tp"),
        P(None, "tp"),
        P("tp", None),
        P(),
        P(),
        P(),
        P(None, "tp"),
        P("tp"),
        P("tp", None),
        P(),
    )
    out_specs = (P(None, "req", "tp"), P(None, "req", None, "tp"))
    return jax.shard_map(
        on_device, mesh=mesh, in_specs=in_specs, out_specs=out_specs, check_vma=False
    )
```

```python
import jax
import jax.numpy as jnp
from jax import lax
from jax.sharding import PartitionSpec as P

HD = 64


def layer_norm(values, scale_row, shift_row):
    average = jnp.mean(values, axis=-1, keepdims=True)
    centred = values - average
    spread = jnp.mean(centred * centred, axis=-1, keepdims=True)
    return centred * lax.rsqrt(spread + 1e-05) * scale_row.astype(jnp.float32) + shift_row.astype(
        jnp.float32
    )


def split_heads(rows_block):
    return rows_block.reshape(rows_block.shape[0], -1, HD)


def block_scores(query_heads, keys_block, allowed):
    scores = jnp.einsum(
        "thd,shd->hts", query_heads, split_heads(keys_block), preferred_element_type=jnp.float32
    )
    return jnp.where(allowed[None], scores, -jnp.inf)


def to_rows(factor):
    return jnp.transpose(factor, (1, 0, 2))


def slot_attention(query_rows, key_rows, value_rows, slot_keys, slot_values, length):
    fresh_len = query_rows.shape[0]
    block_len = min(512, slot_keys.shape[0])
    block_count = slot_keys.shape[0] // block_len
    query_heads = split_heads(query_rows)
    self_mask = jnp.arange(fresh_len)[:, None] >= jnp.arange(fresh_len)[None, :]
    self_scores = block_scores(query_heads, key_rows, self_mask)
    row_top = jnp.max(self_scores, axis=2, keepdims=True)
    raised = jnp.exp(self_scores - row_top)
    row_total = jnp.sum(raised, axis=2, keepdims=True)
    context = jnp.einsum(
        "hts,shd->thd",
        raised.astype(jnp.bfloat16),
        split_heads(value_rows),
        preferred_element_type=jnp.float32,
    )
    positions = jnp.arange(block_len)

    def one_block(number, carry):
        old_top, old_total, running = carry
        begin_at = number * block_len
        keys_block = lax.dynamic_slice_in_dim(slot_keys, begin_at, block_len)
        values_block = lax.dynamic_slice_in_dim(slot_values, begin_at, block_len)
        allowed = jnp.broadcast_to((begin_at + positions < length)[None, :], (fresh_len, block_len))
        scores = block_scores(query_heads, keys_block, allowed)
        new_top = jnp.maximum(old_top, jnp.max(scores, axis=2, keepdims=True))
        factor = jnp.exp(old_top - new_top)
        block_raised = jnp.exp(scores - new_top)
        new_total = old_total * factor + jnp.sum(block_raised, axis=2, keepdims=True)
        added = jnp.einsum(
            "hts,shd->thd",
            block_raised.astype(jnp.bfloat16),
            split_heads(values_block),
            preferred_element_type=jnp.float32,
        )
        return (new_top, new_total, running * to_rows(factor) + added)

    row_top, row_total, context = lax.fori_loop(
        0, block_count, one_block, (row_top, row_total, context)
    )
    context = context / to_rows(row_total)
    return context.reshape(fresh_len, -1).astype(jnp.bfloat16)


def gather_tp(block, tp_count, axis):
    copies = jnp.broadcast_to(
        jnp.expand_dims(block, axis), block.shape[:axis] + (tp_count,) + block.shape[axis:]
    )
    got = lax.all_to_all(copies, "tp", axis, axis, tiled=True)
    return got.reshape(block.shape[:axis] + (-1,) + block.shape[axis + 1 :])


def reduce_tp(partial, tp_count):
    rows = partial.shape[0] // tp_count
    got = lax.all_to_all(partial.reshape(tp_count, rows, -1), "tp", 0, 0, tiled=True)
    return jnp.sum(got.astype(jnp.float32), axis=0)


def on_device(
    hidden_in,
    cache_keys,
    cache_values,
    cache_lengths,
    owner_order,
    request_slot,
    proj_weight,
    proj_bias,
    output_weight,
    output_bias,
    norm_gains,
    norm_biases,
    widen_weight,
    widen_bias,
    narrow_weight,
    narrow_bias,
):
    tp_count = lax.axis_size("tp")
    tp_index = lax.axis_index("tp")
    slot_index = lax.axis_index("req")
    length = cache_lengths[owner_order[slot_index]]
    own_cols = lax.all_to_all(
        hidden_in.at[owner_order].get(mode="promise_in_bounds", unique_indices=True),
        "req",
        split_axis=0,
        concat_axis=1,
        tiled=True,
    )[0]
    fresh_len = own_cols.shape[0]
    width = own_cols.shape[1] * tp_count
    token_rows = gather_tp(own_cols, tp_count, 1)
    projected = (
        jnp.einsum("td,cdf->ctf", token_rows, proj_weight, preferred_element_type=jnp.float32)
        + proj_bias.astype(jnp.float32)[:, None, :]
    )
    query_rows = (projected[0] * HD ** (-0.5)).astype(jnp.bfloat16)
    key_rows = projected[1].astype(jnp.bfloat16)
    value_rows = projected[2].astype(jnp.bfloat16)
    new_cache = jnp.stack([key_rows, value_rows], axis=0)[:, None]
    context = slot_attention(
        query_rows, key_rows, value_rows, cache_keys[0], cache_values[0], length
    )
    rows = fresh_len // tp_count
    own_rows = lax.optimization_barrier(
        lax.dynamic_slice_in_dim(token_rows, tp_index * rows, rows).astype(jnp.float32)
        + output_bias.astype(jnp.float32)
    )
    attended = reduce_tp(
        jnp.dot(context, output_weight, preferred_element_type=jnp.float32).astype(jnp.bfloat16),
        tp_count,
    )
    normed = layer_norm(
        own_rows + attended,
        norm_gains[0],
        norm_biases[0],
    ).astype(jnp.bfloat16)
    normed_all = gather_tp(normed, tp_count, 0)
    widened = jnp.dot(normed_all, widen_weight, preferred_element_type=jnp.float32) + widen_bias.astype(
        jnp.float32
    )
    activated = lax.optimization_barrier(
        jax.nn.gelu(widened, approximate=False).astype(jnp.bfloat16)
    )
    chunk_count = fresh_len // tp_count
    partial = jnp.dot(activated, narrow_weight, preferred_element_type=jnp.float32).astype(
        jnp.bfloat16
    )
    fed_total = reduce_tp(
        jnp.transpose(partial.reshape(chunk_count, tp_count, width), (1, 0, 2)).reshape(
            fresh_len, width
        ),
        tp_count,
    )
    residual = lax.dynamic_index_in_dim(
        normed_all.reshape(chunk_count, tp_count, width), tp_index, 1, keepdims=False
    )
    updated = layer_norm(
        residual.astype(jnp.float32) + fed_total + narrow_bias.astype(jnp.float32),
        norm_gains[1],
        norm_biases[1],
    ).astype(jnp.bfloat16)
    returned = lax.all_to_all(
        updated.reshape(chunk_count * tp_count, width // tp_count),
        ("req", "tp"),
        0,
        0,
        tiled=True,
    ).reshape(-1, tp_count, width // tp_count)
    hidden_out = returned.at[request_slot].get(mode="promise_in_bounds", unique_indices=True)
    return (hidden_out, new_cache)


def solution(mesh):
    in_specs = (
        P(None, "req", "tp"),
        P("req", None, "tp"),
        P("req", None, "tp"),
        P(),
        P(),
        P(),
        P(None, None, "tp"),
        P(None, "tp"),
        P("tp", None),
        P(),
        P(),
        P(),
        P(None, "tp"),
        P("tp"),
        P("tp", None),
        P(),
    )
    out_specs = (P(None, "req", "tp"), P(None, "req", None, "tp"))
    return jax.shard_map(
        on_device, mesh=mesh, in_specs=in_specs, out_specs=out_specs, check_vma=False
    )
```

```python
import jax
import jax.numpy as jnp
from jax import lax
from jax.sharding import PartitionSpec as P

HD = 64


def layer_norm(values, scale_row, shift_row):
    average = jnp.mean(values, axis=-1, keepdims=True)
    centred = values - average
    spread = jnp.mean(centred * centred, axis=-1, keepdims=True)
    return centred * lax.rsqrt(spread + 1e-05) * scale_row.astype(jnp.float32) + shift_row.astype(
        jnp.float32
    )


def split_heads(rows_block):
    return rows_block.reshape(rows_block.shape[0], -1, HD)


def block_scores(query_heads, keys_block, allowed):
    scores = jnp.einsum(
        "thd,shd->hts", query_heads, split_heads(keys_block), preferred_element_type=jnp.float32
    )
    return jnp.where(allowed[None], scores, -jnp.inf)


def to_rows(factor):
    return jnp.transpose(factor, (1, 0, 2))


def slot_attention(query_rows, key_rows, value_rows, slot_keys, slot_values, length, position):
    fresh_len = query_rows.shape[0]
    block_len = min(512, slot_keys.shape[0])
    block_count = slot_keys.shape[0] // block_len
    query_heads = split_heads(query_rows)
    self_mask = position[:, None] >= position[None, :]
    self_scores = block_scores(query_heads, key_rows, self_mask)
    row_top = jnp.max(self_scores, axis=2, keepdims=True)
    raised = jnp.exp(self_scores - row_top)
    row_total = jnp.sum(raised, axis=2, keepdims=True)
    context = jnp.einsum(
        "hts,shd->thd",
        raised.astype(jnp.bfloat16),
        split_heads(value_rows),
        preferred_element_type=jnp.float32,
    )
    positions = jnp.arange(block_len)

    def one_block(number, carry):
        old_top, old_total, running = carry
        begin_at = number * block_len
        keys_block = lax.dynamic_slice_in_dim(slot_keys, begin_at, block_len)
        values_block = lax.dynamic_slice_in_dim(slot_values, begin_at, block_len)
        allowed = jnp.broadcast_to((begin_at + positions < length)[None, :], (fresh_len, block_len))
        scores = block_scores(query_heads, keys_block, allowed)
        new_top = jnp.maximum(old_top, jnp.max(scores, axis=2, keepdims=True))
        factor = jnp.exp(old_top - new_top)
        block_raised = jnp.exp(scores - new_top)
        new_total = old_total * factor + jnp.sum(block_raised, axis=2, keepdims=True)
        added = jnp.einsum(
            "hts,shd->thd",
            block_raised.astype(jnp.bfloat16),
            split_heads(values_block),
            preferred_element_type=jnp.float32,
        )
        return (new_top, new_total, running * to_rows(factor) + added)

    row_top, row_total, context = lax.fori_loop(
        0, block_count, one_block, (row_top, row_total, context)
    )
    context = context / to_rows(row_total)
    return context.reshape(fresh_len, -1).astype(jnp.bfloat16)


def gather_tp(block, tp_count, axis):
    copies = jnp.broadcast_to(
        jnp.expand_dims(block, axis), block.shape[:axis] + (tp_count,) + block.shape[axis:]
    )
    got = lax.all_to_all(copies, "tp", axis, axis, tiled=True)
    return got.reshape(block.shape[:axis] + (-1,) + block.shape[axis + 1 :])


def reduce_tp(partial, tp_count):
    rows = partial.shape[0] // tp_count
    got = lax.all_to_all(partial.reshape(tp_count, rows, -1), "tp", 0, 0, tiled=True)
    return jnp.sum(got.astype(jnp.float32), axis=0)


def on_device(
    hidden_in,
    cache_keys,
    cache_values,
    cache_lengths,
    owner_order,
    request_slot,
    proj_weight,
    proj_bias,
    output_weight,
    output_bias,
    norm_gains,
    norm_biases,
    widen_weight,
    widen_bias,
    narrow_weight,
    narrow_bias,
):
    tp_count = lax.axis_size("tp")
    tp_index = lax.axis_index("tp")
    slot_index = lax.axis_index("req")
    length = cache_lengths[owner_order[slot_index]]
    routed_in = hidden_in.at[owner_order].get(mode="promise_in_bounds", unique_indices=True)
    chunk_len = routed_in.shape[1]
    own_cols = lax.all_to_all(
        jnp.transpose(routed_in, (1, 0, 2)), "req", split_axis=1, concat_axis=1, tiled=True
    )
    chunk_count = own_cols.shape[1]
    own_cols = own_cols.reshape(chunk_len * chunk_count, -1)
    fresh_len = own_cols.shape[0]
    width = own_cols.shape[1] * tp_count
    row_ids = jnp.arange(fresh_len)
    position = (row_ids % chunk_count) * chunk_len + row_ids // chunk_count
    token_rows = gather_tp(own_cols, tp_count, 1)
    projected = (
        jnp.einsum("td,cdf->ctf", token_rows, proj_weight, preferred_element_type=jnp.float32)
        + proj_bias.astype(jnp.float32)[:, None, :]
    )
    query_rows = (projected[0] * HD ** (-0.5)).astype(jnp.bfloat16)
    key_rows = projected[1].astype(jnp.bfloat16)
    value_rows = projected[2].astype(jnp.bfloat16)
    new_cache = jnp.stack([key_rows, value_rows], axis=0).reshape(2, chunk_len, chunk_count, -1)
    new_cache = jnp.transpose(new_cache, (0, 2, 1, 3)).reshape(2, 1, fresh_len, -1)
    context = slot_attention(
        query_rows, key_rows, value_rows, cache_keys[0], cache_values[0], length, position
    )
    rows = fresh_len // tp_count
    own_rows = lax.optimization_barrier(
        lax.dynamic_slice_in_dim(token_rows, tp_index * rows, rows).astype(jnp.float32)
        + output_bias.astype(jnp.float32)
    )
    attended = reduce_tp(
        jnp.dot(context, output_weight, preferred_element_type=jnp.float32).astype(jnp.bfloat16),
        tp_count,
    )
    normed = layer_norm(
        own_rows + attended,
        norm_gains[0],
        norm_biases[0],
    ).astype(jnp.bfloat16)
    normed_all = gather_tp(normed, tp_count, 0)
    widened = jnp.dot(normed_all, widen_weight, preferred_element_type=jnp.float32) + widen_bias.astype(
        jnp.float32
    )
    activated = lax.optimization_barrier(
        jax.nn.gelu(widened, approximate=False).astype(jnp.bfloat16)
    )
    fed_total = reduce_tp(
        jnp.dot(activated, narrow_weight, preferred_element_type=jnp.float32).astype(jnp.bfloat16),
        tp_count,
    )
    updated = layer_norm(
        normed.astype(jnp.float32) + fed_total + narrow_bias.astype(jnp.float32),
        norm_gains[1],
        norm_biases[1],
    ).astype(jnp.bfloat16)
    returned = lax.all_to_all(
        updated.reshape(rows * tp_count, width // tp_count),
        ("req", "tp"),
        0,
        0,
        tiled=True,
    ).reshape(-1, tp_count, width // tp_count)
    hidden_out = returned.at[request_slot].get(mode="promise_in_bounds", unique_indices=True)
    return (hidden_out, new_cache)


def solution(mesh):
    in_specs = (
        P(None, "req", "tp"),
        P("req", None, "tp"),
        P("req", None, "tp"),
        P(),
        P(),
        P(),
        P(None, None, "tp"),
        P(None, "tp"),
        P("tp", None),
        P(),
        P(),
        P(),
        P(None, "tp"),
        P("tp"),
        P("tp", None),
        P(),
    )
    out_specs = (P(None, "req", "tp"), P(None, "req", None, "tp"))
    return jax.shard_map(
        on_device, mesh=mesh, in_specs=in_specs, out_specs=out_specs, check_vma=False
    )
```

```python
import jax
import jax.numpy as jnp
from jax import lax
from jax.sharding import PartitionSpec as P

HD = 64


def layer_norm(values, scale_row, shift_row):
    average = jnp.mean(values, axis=-1, keepdims=True)
    centred = values - average
    spread = jnp.mean(centred * centred, axis=-1, keepdims=True)
    return centred * lax.rsqrt(spread + 1e-05) * scale_row.astype(jnp.float32) + shift_row.astype(
        jnp.float32
    )


def split_heads(rows_block):
    return rows_block.reshape(rows_block.shape[0], -1, HD)


def block_scores(query_heads, keys_block, allowed):
    scores = jnp.einsum(
        "thd,shd->hts", query_heads, split_heads(keys_block), preferred_element_type=jnp.float32
    )
    return jnp.where(allowed[None], scores, -jnp.inf)


def to_rows(factor):
    return jnp.transpose(factor, (1, 0, 2))


def slot_attention(query_rows, key_rows, value_rows, slot_keys, slot_values, length, position):
    fresh_len = query_rows.shape[0]
    block_len = min(512, slot_keys.shape[0])
    block_count = slot_keys.shape[0] // block_len
    query_heads = split_heads(query_rows)
    self_mask = position[:, None] >= position[None, :]
    self_scores = block_scores(query_heads, key_rows, self_mask)
    row_top = jnp.max(self_scores, axis=2, keepdims=True)
    raised = jnp.exp(self_scores - row_top)
    row_total = jnp.sum(raised, axis=2, keepdims=True)
    context = jnp.einsum(
        "hts,shd->thd",
        raised.astype(jnp.bfloat16),
        split_heads(value_rows),
        preferred_element_type=jnp.float32,
    )
    positions = jnp.arange(block_len)

    def one_block(number, carry):
        old_top, old_total, running = carry
        begin_at = number * block_len
        keys_block = lax.dynamic_slice_in_dim(slot_keys, begin_at, block_len)
        values_block = lax.dynamic_slice_in_dim(slot_values, begin_at, block_len)
        allowed = jnp.broadcast_to((begin_at + positions < length)[None, :], (fresh_len, block_len))
        scores = block_scores(query_heads, keys_block, allowed)
        new_top = jnp.maximum(old_top, jnp.max(scores, axis=2, keepdims=True))
        factor = jnp.exp(old_top - new_top)
        block_raised = jnp.exp(scores - new_top)
        new_total = old_total * factor + jnp.sum(block_raised, axis=2, keepdims=True)
        added = jnp.einsum(
            "hts,shd->thd",
            block_raised.astype(jnp.bfloat16),
            split_heads(values_block),
            preferred_element_type=jnp.float32,
        )
        return (new_top, new_total, running * to_rows(factor) + added)

    row_top, row_total, context = lax.fori_loop(
        0, block_count, one_block, (row_top, row_total, context)
    )
    context = context / to_rows(row_total)
    return context.reshape(fresh_len, -1).astype(jnp.bfloat16)


def gather_tp(block, tp_count, axis):
    copies = jnp.broadcast_to(
        jnp.expand_dims(block, axis), block.shape[:axis] + (tp_count,) + block.shape[axis:]
    )
    got = lax.all_to_all(copies, "tp", axis, axis, tiled=True)
    return got.reshape(block.shape[:axis] + (-1,) + block.shape[axis + 1 :])


def reduce_tp(partial, tp_count):
    rows = partial.shape[0] // tp_count
    got = lax.all_to_all(partial.reshape(tp_count, rows, -1), "tp", 0, 0, tiled=True)
    return jnp.sum(got.astype(jnp.float32), axis=0)


def permute_rows(order, table):
    picks = (order[:, None] == jnp.arange(table.shape[0])[None, :]).astype(table.dtype)
    flat = table.reshape(table.shape[0], -1)
    moved = jnp.dot(picks, flat, preferred_element_type=jnp.float32).astype(table.dtype)
    return moved.reshape(table.shape)


def on_device(
    hidden_in,
    cache_keys,
    cache_values,
    cache_lengths,
    owner_order,
    request_slot,
    proj_weight,
    proj_bias,
    output_weight,
    output_bias,
    norm_gains,
    norm_biases,
    widen_weight,
    widen_bias,
    narrow_weight,
    narrow_bias,
):
    tp_count = lax.axis_size("tp")
    tp_index = lax.axis_index("tp")
    slot_index = lax.axis_index("req")
    length = cache_lengths[owner_order[slot_index]]
    routed_in = permute_rows(owner_order, hidden_in)
    chunk_len = routed_in.shape[1]
    own_cols = lax.all_to_all(
        jnp.transpose(routed_in, (1, 0, 2)), "req", split_axis=1, concat_axis=1, tiled=True
    )
    chunk_count = own_cols.shape[1]
    own_cols = own_cols.reshape(chunk_len * chunk_count, -1)
    fresh_len = own_cols.shape[0]
    width = own_cols.shape[1] * tp_count
    row_ids = jnp.arange(fresh_len)
    position = (row_ids % chunk_count) * chunk_len + row_ids // chunk_count
    token_rows = gather_tp(own_cols, tp_count, 1)
    projected = (
        jnp.einsum("td,cdf->ctf", token_rows, proj_weight, preferred_element_type=jnp.float32)
        + proj_bias.astype(jnp.float32)[:, None, :]
    )
    query_rows = (projected[0] * HD ** (-0.5)).astype(jnp.bfloat16)
    key_rows = projected[1].astype(jnp.bfloat16)
    value_rows = projected[2].astype(jnp.bfloat16)
    new_cache = jnp.stack([key_rows, value_rows], axis=0).reshape(2, chunk_len, chunk_count, -1)
    new_cache = jnp.transpose(new_cache, (0, 2, 1, 3)).reshape(2, 1, fresh_len, -1)
    context = slot_attention(
        query_rows, key_rows, value_rows, cache_keys[0], cache_values[0], length, position
    )
    rows = fresh_len // tp_count
    own_rows = lax.optimization_barrier(
        lax.dynamic_slice_in_dim(token_rows, tp_index * rows, rows).astype(jnp.float32)
        + output_bias.astype(jnp.float32)
    )
    attended = reduce_tp(
        jnp.dot(context, output_weight, preferred_element_type=jnp.float32).astype(jnp.bfloat16),
        tp_count,
    )
    normed = layer_norm(
        own_rows + attended,
        norm_gains[0],
        norm_biases[0],
    ).astype(jnp.bfloat16)
    normed_all = gather_tp(normed, tp_count, 0)
    widened = jnp.dot(normed_all, widen_weight, preferred_element_type=jnp.float32) + widen_bias.astype(
        jnp.float32
    )
    activated = lax.optimization_barrier(
        jax.nn.gelu(widened, approximate=False).astype(jnp.bfloat16)
    )
    fed_total = reduce_tp(
        jnp.dot(activated, narrow_weight, preferred_element_type=jnp.float32).astype(jnp.bfloat16),
        tp_count,
    )
    updated = layer_norm(
        normed.astype(jnp.float32) + fed_total + narrow_bias.astype(jnp.float32),
        norm_gains[1],
        norm_biases[1],
    ).astype(jnp.bfloat16)
    returned = lax.all_to_all(
        updated.reshape(rows * tp_count, width // tp_count),
        ("req", "tp"),
        0,
        0,
        tiled=True,
    ).reshape(-1, tp_count, width // tp_count)
    hidden_out = permute_rows(request_slot, returned)
    return (hidden_out, new_cache)


def solution(mesh):
    in_specs = (
        P(None, "req", "tp"),
        P("req", None, "tp"),
        P("req", None, "tp"),
        P(),
        P(),
        P(),
        P(None, None, "tp"),
        P(None, "tp"),
        P("tp", None),
        P(),
        P(),
        P(),
        P(None, "tp"),
        P("tp"),
        P("tp", None),
        P(),
    )
    out_specs = (P(None, "req", "tp"), P(None, "req", None, "tp"))
    return jax.shard_map(
        on_device, mesh=mesh, in_specs=in_specs, out_specs=out_specs, check_vma=False
    )
```

```python
import jax
import jax.numpy as jnp
from jax import lax
from jax.sharding import Mesh, PartitionSpec as P

HD = 64


def layer_norm(values, scale_row, shift_row):
    average = jnp.mean(values, axis=-1, keepdims=True)
    centred = values - average
    spread = jnp.mean(centred * centred, axis=-1, keepdims=True)
    return centred * lax.rsqrt(spread + 1e-05) * scale_row.astype(jnp.float32) + shift_row.astype(
        jnp.float32
    )


def split_heads(rows_block):
    return rows_block.reshape(rows_block.shape[0], -1, HD)


def block_scores(query_heads, keys_block, allowed):
    scores = jnp.einsum(
        "thd,shd->hts", query_heads, split_heads(keys_block), preferred_element_type=jnp.float32
    )
    return jnp.where(allowed[None], scores, -jnp.inf)


def to_rows(factor):
    return jnp.transpose(factor, (1, 0, 2))


def slot_attention(query_rows, key_rows, value_rows, slot_keys, slot_values, length, position):
    fresh_len = query_rows.shape[0]
    block_len = min(512, slot_keys.shape[0])
    block_count = slot_keys.shape[0] // block_len
    query_heads = split_heads(query_rows)
    self_mask = position[:, None] >= position[None, :]
    self_scores = block_scores(query_heads, key_rows, self_mask)
    row_top = jnp.max(self_scores, axis=2, keepdims=True)
    raised = jnp.exp(self_scores - row_top)
    row_total = jnp.sum(raised, axis=2, keepdims=True)
    context = jnp.einsum(
        "hts,shd->thd",
        raised.astype(jnp.bfloat16),
        split_heads(value_rows),
        preferred_element_type=jnp.float32,
    )
    positions = jnp.arange(block_len)

    def one_block(number, carry):
        old_top, old_total, running = carry
        begin_at = number * block_len
        keys_block = lax.dynamic_slice_in_dim(slot_keys, begin_at, block_len)
        values_block = lax.dynamic_slice_in_dim(slot_values, begin_at, block_len)
        allowed = jnp.broadcast_to((begin_at + positions < length)[None, :], (fresh_len, block_len))
        scores = block_scores(query_heads, keys_block, allowed)
        new_top = jnp.maximum(old_top, jnp.max(scores, axis=2, keepdims=True))
        factor = jnp.exp(old_top - new_top)
        block_raised = jnp.exp(scores - new_top)
        new_total = old_total * factor + jnp.sum(block_raised, axis=2, keepdims=True)
        added = jnp.einsum(
            "hts,shd->thd",
            block_raised.astype(jnp.bfloat16),
            split_heads(values_block),
            preferred_element_type=jnp.float32,
        )
        return (new_top, new_total, running * to_rows(factor) + added)

    row_top, row_total, context = lax.fori_loop(
        0, block_count, one_block, (row_top, row_total, context)
    )
    context = context / to_rows(row_total)
    return context.reshape(fresh_len, -1).astype(jnp.bfloat16)


TP = ("x", "core")


def gather_tp(block, tp_count, axis, names=TP):
    copies = jnp.broadcast_to(
        jnp.expand_dims(block, axis), block.shape[:axis] + (tp_count,) + block.shape[axis:]
    )
    got = lax.all_to_all(copies, names, axis, axis, tiled=True)
    return got.reshape(block.shape[:axis] + (-1,) + block.shape[axis + 1 :])


def reduce_tp(partial, tp_count, names=TP):
    rows = partial.shape[0] // tp_count
    got = lax.all_to_all(partial.reshape(tp_count, rows, -1), names, 0, 0, tiled=True)
    return jnp.sum(got.astype(jnp.float32), axis=0)


def from_partner(block):
    return lax.ppermute(block, "core", [(0, 1), (1, 0)])


def permute_rows(order, table):
    picks = (order[:, None] == jnp.arange(table.shape[0])[None, :]).astype(table.dtype)
    flat = table.reshape(table.shape[0], -1)
    moved = jnp.dot(picks, flat, preferred_element_type=jnp.float32).astype(table.dtype)
    return moved.reshape(table.shape)


def on_device(
    hidden_in,
    cache_keys,
    cache_values,
    cache_lengths,
    owner_order,
    request_slot,
    proj_weight,
    proj_bias,
    output_weight,
    output_bias,
    norm_gains,
    norm_biases,
    widen_weight,
    widen_bias,
    narrow_weight,
    narrow_bias,
):
    x_count = lax.axis_size("x")
    tp_count = x_count * lax.axis_size("core")
    tp_index = lax.axis_index(TP)
    partner_widen = from_partner(widen_weight)
    partner_widen_bias = from_partner(widen_bias)
    partner_narrow = from_partner(narrow_weight)
    slot_index = lax.axis_index("req")
    length = cache_lengths[owner_order[slot_index]]
    routed_in = permute_rows(owner_order, hidden_in)
    chunk_len = routed_in.shape[1]
    own_cols = lax.all_to_all(
        jnp.transpose(routed_in, (1, 0, 2)), "req", split_axis=1, concat_axis=1, tiled=True
    )
    chunk_count = own_cols.shape[1]
    own_cols = own_cols.reshape(chunk_len * chunk_count, -1)
    fresh_len = own_cols.shape[0]
    width = own_cols.shape[1] * tp_count
    row_ids = jnp.arange(fresh_len)
    position = (row_ids % chunk_count) * chunk_len + row_ids // chunk_count
    token_rows = gather_tp(own_cols, tp_count, 1)
    projected = (
        jnp.einsum("td,cdf->ctf", token_rows, proj_weight, preferred_element_type=jnp.float32)
        + proj_bias.astype(jnp.float32)[:, None, :]
    )
    query_rows = (projected[0] * HD ** (-0.5)).astype(jnp.bfloat16)
    key_rows = projected[1].astype(jnp.bfloat16)
    value_rows = projected[2].astype(jnp.bfloat16)
    new_cache = jnp.stack([key_rows, value_rows], axis=0).reshape(2, chunk_len, chunk_count, -1)
    new_cache = jnp.transpose(new_cache, (0, 2, 1, 3)).reshape(2, 1, fresh_len, -1)
    context = slot_attention(
        query_rows, key_rows, value_rows, cache_keys[0], cache_values[0], length, position
    )
    rows = fresh_len // tp_count
    own_rows = lax.optimization_barrier(
        lax.dynamic_slice_in_dim(token_rows, tp_index * rows, rows).astype(jnp.float32)
        + output_bias.astype(jnp.float32)
    )
    attended = reduce_tp(
        jnp.dot(context, output_weight, preferred_element_type=jnp.float32).astype(jnp.bfloat16),
        tp_count,
    )
    normed = layer_norm(
        own_rows + attended,
        norm_gains[0],
        norm_biases[0],
    ).astype(jnp.bfloat16)
    normed_half = gather_tp(normed, x_count, 0, "x")

    def unit_group(widen_block, bias_block, narrow_block):
        widened = jnp.dot(normed_half, widen_block, preferred_element_type=jnp.float32)
        activated = jax.nn.gelu(
            widened + bias_block.astype(jnp.float32), approximate=False
        ).astype(jnp.bfloat16)
        partial = jnp.dot(activated, narrow_block, preferred_element_type=jnp.float32)
        return partial.astype(jnp.bfloat16).astype(jnp.float32)

    pair = unit_group(widen_weight, widen_bias, narrow_weight) + unit_group(
        partner_widen, partner_widen_bias, partner_narrow
    )
    fed_total = reduce_tp(pair.astype(jnp.bfloat16), x_count, "x")
    updated = layer_norm(
        normed.astype(jnp.float32) + fed_total + narrow_bias.astype(jnp.float32),
        norm_gains[1],
        norm_biases[1],
    ).astype(jnp.bfloat16)
    returned = lax.all_to_all(
        updated.reshape(rows * tp_count, width // tp_count),
        ("req",) + TP,
        0,
        0,
        tiled=True,
    ).reshape(-1, tp_count, width // tp_count)
    hidden_out = permute_rows(request_slot, returned)
    return (hidden_out, new_cache)


def solution(mesh):
    req_count, tp_count = mesh.devices.shape
    split = Mesh(mesh.devices.reshape(req_count, tp_count // 2, 2), ("req",) + TP)
    in_specs = (
        P(None, "req", TP),
        P("req", None, TP),
        P("req", None, TP),
        P(),
        P(),
        P(),
        P(None, None, TP),
        P(None, TP),
        P(TP, None),
        P(),
        P(),
        P(),
        P(None, TP),
        P(TP),
        P(TP, None),
        P(),
    )
    out_specs = (P(None, "req", TP), P(None, "req", None, TP))
    return jax.shard_map(
        on_device, mesh=split, in_specs=in_specs, out_specs=out_specs, check_vma=False
    )
```

```python
import jax
import jax.numpy as jnp
from jax import lax
from jax.sharding import Mesh, PartitionSpec as P

HD = 64


def layer_norm(values, scale_row, shift_row):
    average = jnp.mean(values, axis=-1, keepdims=True)
    centred = values - average
    spread = jnp.mean(centred * centred, axis=-1, keepdims=True)
    return centred * lax.rsqrt(spread + 1e-05) * scale_row.astype(jnp.float32) + shift_row.astype(
        jnp.float32
    )


def split_heads(rows_block):
    return rows_block.reshape(rows_block.shape[0], -1, HD)


def block_scores(query_heads, keys_block, allowed):
    scores = jnp.einsum(
        "thd,shd->hts", query_heads, split_heads(keys_block), preferred_element_type=jnp.float32
    )
    return jnp.where(allowed[None], scores, -jnp.inf)


def to_rows(factor):
    return jnp.transpose(factor, (1, 0, 2))


def slot_attention(query_rows, key_rows, value_rows, slot_keys, slot_values, length, position):
    fresh_len = query_rows.shape[0]
    block_len = min(512, slot_keys.shape[0])
    block_count = slot_keys.shape[0] // block_len
    query_heads = split_heads(query_rows)
    self_mask = position[:, None] >= position[None, :]
    self_scores = block_scores(query_heads, key_rows, self_mask)
    row_top = jnp.max(self_scores, axis=2, keepdims=True)
    raised = jnp.exp(self_scores - row_top)
    row_total = jnp.sum(raised, axis=2, keepdims=True)
    context = jnp.einsum(
        "hts,shd->thd",
        raised.astype(jnp.bfloat16),
        split_heads(value_rows),
        preferred_element_type=jnp.float32,
    )
    positions = jnp.arange(block_len)

    def one_block(number, carry):
        old_top, old_total, running = carry
        begin_at = number * block_len
        keys_block = lax.dynamic_slice_in_dim(slot_keys, begin_at, block_len)
        values_block = lax.dynamic_slice_in_dim(slot_values, begin_at, block_len)
        allowed = jnp.broadcast_to((begin_at + positions < length)[None, :], (fresh_len, block_len))
        scores = block_scores(query_heads, keys_block, allowed)
        new_top = jnp.maximum(old_top, jnp.max(scores, axis=2, keepdims=True))
        factor = jnp.exp(old_top - new_top)
        block_raised = jnp.exp(scores - new_top)
        new_total = old_total * factor + jnp.sum(block_raised, axis=2, keepdims=True)
        added = jnp.einsum(
            "hts,shd->thd",
            block_raised.astype(jnp.bfloat16),
            split_heads(values_block),
            preferred_element_type=jnp.float32,
        )
        return (new_top, new_total, running * to_rows(factor) + added)

    row_top, row_total, context = lax.fori_loop(
        0, block_count, one_block, (row_top, row_total, context)
    )
    context = context / to_rows(row_total)
    return context.reshape(fresh_len, -1).astype(jnp.bfloat16)


TP = ("x", "core")


def gather_tp(block, tp_count, axis, names=TP):
    copies = jnp.broadcast_to(
        jnp.expand_dims(block, axis), block.shape[:axis] + (tp_count,) + block.shape[axis:]
    )
    got = lax.all_to_all(copies, names, axis, axis, tiled=True)
    return got.reshape(block.shape[:axis] + (-1,) + block.shape[axis + 1 :])


def reduce_tp(partial, tp_count, names=TP):
    rows = partial.shape[0] // tp_count
    got = lax.all_to_all(partial.reshape(tp_count, rows, -1), names, 0, 0, tiled=True)
    return jnp.sum(got.astype(jnp.float32), axis=0)


def from_partner(block):
    return lax.ppermute(block, "core", [(0, 1), (1, 0)])


def permute_rows(order, table):
    picks = (order[:, None] == jnp.arange(table.shape[0])[None, :]).astype(table.dtype)
    flat = table.reshape(table.shape[0], -1)
    moved = jnp.dot(picks, flat, preferred_element_type=jnp.float32).astype(table.dtype)
    return moved.reshape(table.shape)


def on_device(
    hidden_in,
    cache_keys,
    cache_values,
    cache_lengths,
    owner_order,
    request_slot,
    proj_weight,
    proj_bias,
    output_weight,
    output_bias,
    norm_gains,
    norm_biases,
    widen_weight,
    widen_bias,
    narrow_weight,
    narrow_bias,
):
    x_count = lax.axis_size("x")
    tp_count = x_count * lax.axis_size("core")
    tp_index = lax.axis_index(TP)
    partner_widen = from_partner(widen_weight)
    partner_widen_bias = from_partner(widen_bias)
    partner_narrow = from_partner(narrow_weight)
    partner_output = from_partner(output_weight)
    core_index = lax.axis_index("core")
    slot_index = lax.axis_index("req")
    length = cache_lengths[owner_order[slot_index]]
    routed_in = permute_rows(owner_order, hidden_in)
    chunk_len = routed_in.shape[1]
    own_cols = lax.all_to_all(
        jnp.transpose(routed_in, (1, 0, 2)), "req", split_axis=1, concat_axis=1, tiled=True
    )
    chunk_count = own_cols.shape[1]
    own_cols = own_cols.reshape(chunk_len * chunk_count, -1)
    fresh_len = own_cols.shape[0]
    width = own_cols.shape[1] * tp_count
    row_ids = jnp.arange(fresh_len)
    position = (row_ids % chunk_count) * chunk_len + row_ids // chunk_count
    token_rows = gather_tp(own_cols, tp_count, 1)
    projected = (
        jnp.einsum("td,cdf->ctf", token_rows, proj_weight, preferred_element_type=jnp.float32)
        + proj_bias.astype(jnp.float32)[:, None, :]
    )
    query_rows = (projected[0] * HD ** (-0.5)).astype(jnp.bfloat16)
    key_rows = projected[1].astype(jnp.bfloat16)
    value_rows = projected[2].astype(jnp.bfloat16)
    new_cache = jnp.stack([key_rows, value_rows], axis=0).reshape(2, chunk_len, chunk_count, -1)
    new_cache = jnp.transpose(new_cache, (0, 2, 1, 3)).reshape(2, 1, fresh_len, -1)
    context = slot_attention(
        query_rows, key_rows, value_rows, cache_keys[0], cache_values[0], length, position
    )
    rows = fresh_len // tp_count
    own_rows = lax.optimization_barrier(
        lax.dynamic_slice_in_dim(token_rows, tp_index * rows, rows).astype(jnp.float32)
        + output_bias.astype(jnp.float32)
    )
    halves = context.reshape(x_count, 2, rows, -1)
    kept = lax.dynamic_index_in_dim(halves, core_index, 1, keepdims=False)
    sent = lax.dynamic_index_in_dim(halves, 1 - core_index, 1, keepdims=False)
    got = from_partner(sent)

    def head_group(context_rows, weight_block):
        partial = jnp.dot(
            context_rows.reshape(x_count * rows, -1), weight_block, preferred_element_type=jnp.float32
        )
        return partial.astype(jnp.bfloat16).astype(jnp.float32)

    attended = reduce_tp(
        (head_group(kept, output_weight) + head_group(got, partner_output)).astype(jnp.bfloat16),
        x_count,
        "x",
    )
    normed = layer_norm(
        own_rows + attended,
        norm_gains[0],
        norm_biases[0],
    ).astype(jnp.bfloat16)
    normed_half = gather_tp(normed, x_count, 0, "x")

    def unit_group(widen_block, bias_block, narrow_block):
        widened = jnp.dot(normed_half, widen_block, preferred_element_type=jnp.float32)
        activated = jax.nn.gelu(
            widened + bias_block.astype(jnp.float32), approximate=False
        ).astype(jnp.bfloat16)
        partial = jnp.dot(activated, narrow_block, preferred_element_type=jnp.float32)
        return partial.astype(jnp.bfloat16).astype(jnp.float32)

    pair = unit_group(widen_weight, widen_bias, narrow_weight) + unit_group(
        partner_widen, partner_widen_bias, partner_narrow
    )
    fed_total = reduce_tp(pair.astype(jnp.bfloat16), x_count, "x")
    updated = layer_norm(
        normed.astype(jnp.float32) + fed_total + narrow_bias.astype(jnp.float32),
        norm_gains[1],
        norm_biases[1],
    ).astype(jnp.bfloat16)
    returned = lax.all_to_all(
        updated.reshape(rows * tp_count, width // tp_count),
        ("req",) + TP,
        0,
        0,
        tiled=True,
    ).reshape(-1, tp_count, width // tp_count)
    hidden_out = permute_rows(request_slot, returned)
    return (hidden_out, new_cache)


def solution(mesh):
    req_count, tp_count = mesh.devices.shape
    split = Mesh(mesh.devices.reshape(req_count, tp_count // 2, 2), ("req",) + TP)
    in_specs = (
        P(None, "req", TP),
        P("req", None, TP),
        P("req", None, TP),
        P(),
        P(),
        P(),
        P(None, None, TP),
        P(None, TP),
        P(TP, None),
        P(),
        P(),
        P(),
        P(None, TP),
        P(TP),
        P(TP, None),
        P(),
    )
    out_specs = (P(None, "req", TP), P(None, "req", None, TP))
    return jax.shard_map(
        on_device, mesh=split, in_specs=in_specs, out_specs=out_specs, check_vma=False
    )
```

```python
import jax
import jax.numpy as jnp
from jax import lax
from jax.sharding import Mesh, PartitionSpec as P

HD = 64


def layer_norm(values, scale_row, shift_row):
    average = jnp.mean(values, axis=-1, keepdims=True)
    centred = values - average
    spread = jnp.mean(centred * centred, axis=-1, keepdims=True)
    return centred * lax.rsqrt(spread + 1e-05) * scale_row.astype(jnp.float32) + shift_row.astype(
        jnp.float32
    )


def split_heads(rows_block):
    return rows_block.reshape(rows_block.shape[0], -1, HD)


def block_scores(query_heads, keys_block, allowed):
    scores = jnp.einsum(
        "thd,shd->hts", query_heads, split_heads(keys_block), preferred_element_type=jnp.float32
    )
    return jnp.where(allowed[None], scores, -jnp.inf)


def to_rows(factor):
    return jnp.transpose(factor, (1, 0, 2))


def slot_attention(query_rows, key_rows, value_rows, slot_keys, slot_values, length, position):
    fresh_len = query_rows.shape[0]
    block_len = min(512, slot_keys.shape[0])
    block_count = slot_keys.shape[0] // block_len
    query_heads = split_heads(query_rows)
    self_mask = position[:, None] >= position[None, :]
    self_scores = block_scores(query_heads, key_rows, self_mask)
    row_top = jnp.max(self_scores, axis=2, keepdims=True)
    raised = jnp.exp(self_scores - row_top)
    row_total = jnp.sum(raised, axis=2, keepdims=True)
    context = jnp.einsum(
        "hts,shd->thd",
        raised.astype(jnp.bfloat16),
        split_heads(value_rows),
        preferred_element_type=jnp.float32,
    )
    positions = jnp.arange(block_len)

    def one_block(number, carry):
        old_top, old_total, running = carry
        begin_at = number * block_len
        keys_block = lax.dynamic_slice_in_dim(slot_keys, begin_at, block_len)
        values_block = lax.dynamic_slice_in_dim(slot_values, begin_at, block_len)
        allowed = jnp.broadcast_to((begin_at + positions < length)[None, :], (fresh_len, block_len))
        scores = block_scores(query_heads, keys_block, allowed)
        new_top = jnp.maximum(old_top, jnp.max(scores, axis=2, keepdims=True))
        factor = jnp.exp(old_top - new_top)
        block_raised = jnp.exp(scores - new_top)
        new_total = old_total * factor + jnp.sum(block_raised, axis=2, keepdims=True)
        added = jnp.einsum(
            "hts,shd->thd",
            block_raised.astype(jnp.bfloat16),
            split_heads(values_block),
            preferred_element_type=jnp.float32,
        )
        return (new_top, new_total, running * to_rows(factor) + added)

    row_top, row_total, context = lax.fori_loop(
        0, block_count, one_block, (row_top, row_total, context)
    )
    context = context / to_rows(row_total)
    return context.reshape(fresh_len, -1).astype(jnp.bfloat16)


TP = ("x", "core")


def gather_tp(block, tp_count, axis, names=TP):
    copies = jnp.broadcast_to(
        jnp.expand_dims(block, axis), block.shape[:axis] + (tp_count,) + block.shape[axis:]
    )
    got = lax.all_to_all(copies, names, axis, axis, tiled=True)
    return got.reshape(block.shape[:axis] + (-1,) + block.shape[axis + 1 :])


def reduce_tp(partial, tp_count, names=TP):
    rows = partial.shape[0] // tp_count
    got = lax.all_to_all(partial.reshape(tp_count, rows, -1), names, 0, 0, tiled=True)
    return jnp.sum(got.astype(jnp.float32), axis=0)


def from_partner(block):
    return lax.ppermute(block, "core", [(0, 1), (1, 0)])


def permute_rows(order, table):
    picks = (order[:, None] == jnp.arange(table.shape[0])[None, :]).astype(table.dtype)
    flat = table.reshape(table.shape[0], -1)
    moved = jnp.dot(picks, flat, preferred_element_type=jnp.float32).astype(table.dtype)
    return moved.reshape(table.shape)


def on_device(
    hidden_in,
    cache_keys,
    cache_values,
    cache_lengths,
    owner_order,
    request_slot,
    proj_weight,
    proj_bias,
    output_weight,
    output_bias,
    norm_gains,
    norm_biases,
    widen_weight,
    widen_bias,
    narrow_weight,
    narrow_bias,
):
    x_count = lax.axis_size("x")
    tp_count = x_count * lax.axis_size("core")
    tp_index = lax.axis_index(TP)
    partner_widen = from_partner(widen_weight)
    partner_widen_bias = from_partner(widen_bias)
    partner_narrow = from_partner(narrow_weight)
    partner_output = from_partner(output_weight)
    core_index = lax.axis_index("core")
    slot_index = lax.axis_index("req")
    length = cache_lengths[owner_order[slot_index]]
    routed_in = permute_rows(owner_order, hidden_in)
    chunk_len = routed_in.shape[1]
    own_cols = lax.all_to_all(
        jnp.transpose(routed_in, (1, 0, 2)), "req", split_axis=1, concat_axis=1, tiled=True
    )
    chunk_count = own_cols.shape[1]
    own_cols = own_cols.reshape(chunk_len * chunk_count, -1)
    fresh_len = own_cols.shape[0]
    width = own_cols.shape[1] * tp_count
    row_ids = jnp.arange(fresh_len)
    position = (row_ids % chunk_count) * chunk_len + row_ids // chunk_count
    token_rows = gather_tp(own_cols, tp_count, 1)
    projected = (
        jnp.einsum("td,cdf->ctf", token_rows, proj_weight, preferred_element_type=jnp.float32)
        + proj_bias.astype(jnp.float32)[:, None, :]
    )
    query_rows = (projected[0] * HD ** (-0.5)).astype(jnp.bfloat16)
    key_rows = projected[1].astype(jnp.bfloat16)
    value_rows = projected[2].astype(jnp.bfloat16)
    new_cache = jnp.stack([key_rows, value_rows], axis=0).reshape(2, chunk_len, chunk_count, -1)
    new_cache = jnp.transpose(new_cache, (0, 2, 1, 3)).reshape(2, 1, fresh_len, -1)
    context = slot_attention(
        query_rows, key_rows, value_rows, cache_keys[0], cache_values[0], length, position
    )
    rows = fresh_len // tp_count
    own_rows = lax.optimization_barrier(
        lax.dynamic_slice_in_dim(token_rows, tp_index * rows, rows).astype(jnp.float32)
        + output_bias.astype(jnp.float32)
    )
    halves = context.reshape(x_count, 2, rows, -1)
    kept = lax.dynamic_index_in_dim(halves, core_index, 1, keepdims=False)
    sent = lax.dynamic_index_in_dim(halves, 1 - core_index, 1, keepdims=False)
    got = from_partner(sent)

    def head_group(context_rows, weight_block):
        partial = jnp.dot(
            context_rows.reshape(x_count * rows, -1), weight_block, preferred_element_type=jnp.float32
        )
        return partial.astype(jnp.bfloat16).astype(jnp.float32)

    attended = reduce_tp(
        (head_group(kept, output_weight) + head_group(got, partner_output)).astype(jnp.bfloat16),
        x_count,
        "x",
    )
    normed = layer_norm(
        own_rows + attended,
        norm_gains[0],
        norm_biases[0],
    ).astype(jnp.bfloat16)
    normed_half = gather_tp(normed, x_count, 0, "x")

    unit_count = widen_weight.shape[1]
    widened = jnp.dot(
        normed_half,
        jnp.concatenate([widen_weight, partner_widen], axis=1),
        preferred_element_type=jnp.float32,
    ) + jnp.concatenate([widen_bias, partner_widen_bias]).astype(jnp.float32)
    activated = lax.optimization_barrier(
        jax.nn.gelu(widened, approximate=False).astype(jnp.bfloat16)
    )

    def unit_group(activated_block, narrow_block):
        partial = jnp.dot(activated_block, narrow_block, preferred_element_type=jnp.float32)
        return partial.astype(jnp.bfloat16).astype(jnp.float32)

    pair = unit_group(activated[:, :unit_count], narrow_weight) + unit_group(
        activated[:, unit_count:], partner_narrow
    )
    fed_total = reduce_tp(pair.astype(jnp.bfloat16), x_count, "x")
    updated = layer_norm(
        normed.astype(jnp.float32) + fed_total + narrow_bias.astype(jnp.float32),
        norm_gains[1],
        norm_biases[1],
    ).astype(jnp.bfloat16)
    returned = lax.all_to_all(
        updated.reshape(rows * tp_count, width // tp_count),
        ("req",) + TP,
        0,
        0,
        tiled=True,
    ).reshape(-1, tp_count, width // tp_count)
    hidden_out = permute_rows(request_slot, returned)
    return (hidden_out, new_cache)


def solution(mesh):
    req_count, tp_count = mesh.devices.shape
    split = Mesh(mesh.devices.reshape(req_count, tp_count // 2, 2), ("req",) + TP)
    in_specs = (
        P(None, "req", TP),
        P("req", None, TP),
        P("req", None, TP),
        P(),
        P(),
        P(),
        P(None, None, TP),
        P(None, TP),
        P(TP, None),
        P(),
        P(),
        P(),
        P(None, TP),
        P(TP),
        P(TP, None),
        P(),
    )
    out_specs = (P(None, "req", TP), P(None, "req", None, TP))
    return jax.shard_map(
        on_device, mesh=split, in_specs=in_specs, out_specs=out_specs, check_vma=False
    )
```

```python
import jax
import jax.numpy as jnp
from jax import lax
from jax.sharding import Mesh, PartitionSpec as P

HD = 64


def layer_norm(values, scale_row, shift_row):
    average = jnp.mean(values, axis=-1, keepdims=True)
    centred = values - average
    spread = jnp.mean(centred * centred, axis=-1, keepdims=True)
    return centred * lax.rsqrt(spread + 1e-05) * scale_row.astype(jnp.float32) + shift_row.astype(
        jnp.float32
    )


def split_heads(rows_block):
    return rows_block.reshape(rows_block.shape[0], -1, HD)


def block_scores(query_heads, keys_block, allowed):
    scores = jnp.einsum(
        "thd,shd->hts", query_heads, split_heads(keys_block), preferred_element_type=jnp.float32
    )
    return jnp.where(allowed[None], scores, -jnp.inf)


def to_rows(factor):
    return jnp.transpose(factor, (1, 0, 2))


def slot_attention(query_rows, key_rows, value_rows, slot_keys, slot_values, length, position):
    fresh_len = query_rows.shape[0]
    block_len = min(512, slot_keys.shape[0])
    block_count = slot_keys.shape[0] // block_len
    query_heads = split_heads(query_rows)
    self_mask = position[:, None] >= position[None, :]
    self_scores = block_scores(query_heads, key_rows, self_mask)
    row_top = jnp.max(self_scores, axis=2, keepdims=True)
    raised = jnp.exp(self_scores - row_top)
    row_total = jnp.sum(raised, axis=2, keepdims=True)
    context = jnp.einsum(
        "hts,shd->thd",
        raised.astype(jnp.bfloat16),
        split_heads(value_rows),
        preferred_element_type=jnp.float32,
    )
    positions = jnp.arange(block_len)

    def one_block(number, carry):
        old_top, old_total, running = carry
        begin_at = number * block_len
        keys_block = lax.dynamic_slice_in_dim(slot_keys, begin_at, block_len)
        values_block = lax.dynamic_slice_in_dim(slot_values, begin_at, block_len)
        allowed = jnp.broadcast_to((begin_at + positions < length)[None, :], (fresh_len, block_len))
        scores = block_scores(query_heads, keys_block, allowed)
        new_top = jnp.maximum(old_top, jnp.max(scores, axis=2, keepdims=True))
        factor = jnp.exp(old_top - new_top)
        block_raised = jnp.exp(scores - new_top)
        new_total = old_total * factor + jnp.sum(block_raised, axis=2, keepdims=True)
        added = jnp.einsum(
            "hts,shd->thd",
            block_raised.astype(jnp.bfloat16),
            split_heads(values_block),
            preferred_element_type=jnp.float32,
        )
        return (new_top, new_total, running * to_rows(factor) + added)

    row_top, row_total, context = lax.fori_loop(
        0, block_count, one_block, (row_top, row_total, context)
    )
    context = context / to_rows(row_total)
    return context.reshape(fresh_len, -1).astype(jnp.bfloat16)


TP = ("x", "core")


def gather_tp(block, tp_count, axis, names=TP):
    copies = jnp.broadcast_to(
        jnp.expand_dims(block, axis), block.shape[:axis] + (tp_count,) + block.shape[axis:]
    )
    got = lax.all_to_all(copies, names, axis, axis, tiled=True)
    return got.reshape(block.shape[:axis] + (-1,) + block.shape[axis + 1 :])


def reduce_tp(partial, tp_count, names=TP):
    rows = partial.shape[0] // tp_count
    got = lax.all_to_all(partial.reshape(tp_count, rows, -1), names, 0, 0, tiled=True)
    return jnp.sum(got.astype(jnp.float32), axis=0)


def from_partner(block):
    return lax.ppermute(block, "core", [(0, 1), (1, 0)])


def permute_rows(order, table):
    picks = (order[:, None] == jnp.arange(table.shape[0])[None, :]).astype(table.dtype)
    flat = table.reshape(table.shape[0], -1)
    moved = jnp.dot(picks, flat, preferred_element_type=jnp.float32).astype(table.dtype)
    return moved.reshape(table.shape)


def on_device(
    hidden_in,
    cache_keys,
    cache_values,
    cache_lengths,
    owner_order,
    request_slot,
    proj_weight,
    proj_bias,
    output_weight,
    output_bias,
    norm_gains,
    norm_biases,
    widen_weight,
    widen_bias,
    narrow_weight,
    narrow_bias,
):
    x_count = lax.axis_size("x")
    tp_count = x_count * lax.axis_size("core")
    tp_index = lax.axis_index(TP)
    partner_widen = from_partner(widen_weight)
    partner_widen_bias = from_partner(widen_bias)
    partner_narrow = from_partner(narrow_weight)
    partner_output = from_partner(output_weight)
    core_index = lax.axis_index("core")
    slot_index = lax.axis_index("req")
    length = cache_lengths[owner_order[slot_index]]
    routed_in = permute_rows(owner_order, hidden_in)
    chunk_len = routed_in.shape[1]
    own_cols = lax.all_to_all(
        jnp.transpose(routed_in, (1, 0, 2)), "req", split_axis=1, concat_axis=1, tiled=True
    )
    chunk_count = own_cols.shape[1]
    own_cols = own_cols.reshape(chunk_len * chunk_count, -1)
    fresh_len = own_cols.shape[0]
    width = own_cols.shape[1] * tp_count
    row_ids = jnp.arange(fresh_len)
    position = (row_ids % chunk_count) * chunk_len + row_ids // chunk_count
    token_rows = gather_tp(own_cols, tp_count, 1)
    projected = (
        jnp.einsum("td,cdf->ctf", token_rows, proj_weight, preferred_element_type=jnp.float32)
        + proj_bias.astype(jnp.float32)[:, None, :]
    )
    query_rows = (projected[0] * HD ** (-0.5)).astype(jnp.bfloat16)
    key_rows = projected[1].astype(jnp.bfloat16)
    value_rows = projected[2].astype(jnp.bfloat16)
    new_cache = jnp.stack([key_rows, value_rows], axis=0).reshape(2, chunk_len, chunk_count, -1)
    new_cache = jnp.transpose(new_cache, (0, 2, 1, 3)).reshape(2, 1, fresh_len, -1)
    context = slot_attention(
        query_rows, key_rows, value_rows, cache_keys[0], cache_values[0], length, position
    )
    rows = fresh_len // tp_count
    own_rows = lax.optimization_barrier(
        lax.dynamic_slice_in_dim(token_rows, tp_index * rows, rows).astype(jnp.float32)
        + output_bias.astype(jnp.float32)
    )
    halves = context.reshape(x_count, 2, rows, -1)
    kept = lax.dynamic_index_in_dim(halves, core_index, 1, keepdims=False)
    sent = lax.dynamic_index_in_dim(halves, 1 - core_index, 1, keepdims=False)
    got = from_partner(sent)

    def head_group(context_rows, weight_block):
        partial = jnp.dot(
            context_rows.reshape(x_count * rows, -1), weight_block, preferred_element_type=jnp.float32
        )
        return partial.astype(jnp.bfloat16).astype(jnp.float32)

    attended = reduce_tp(
        (head_group(kept, output_weight) + head_group(got, partner_output)).astype(jnp.bfloat16),
        x_count,
        "x",
    )
    pre_norm = own_rows + attended
    average = jnp.mean(pre_norm, axis=-1, keepdims=True)
    centred = pre_norm - average
    spread = jnp.mean(centred * centred, axis=-1, keepdims=True)
    normed_copies = (
        jnp.broadcast_to(centred[None], (x_count,) + centred.shape)
        * lax.rsqrt(spread + 1e-05)
        * norm_gains[0].astype(jnp.float32)
        + norm_biases[0].astype(jnp.float32)
    ).astype(jnp.bfloat16)
    normed = normed_copies[0]
    normed_half = lax.all_to_all(normed_copies, "x", 0, 0, tiled=True).reshape(-1, width)
    unit_count = widen_weight.shape[1]
    widened = jnp.dot(
        normed_half,
        jnp.concatenate([widen_weight, partner_widen], axis=1),
        preferred_element_type=jnp.float32,
    ) + jnp.concatenate([widen_bias, partner_widen_bias]).astype(jnp.float32)
    activated = lax.optimization_barrier(
        jax.nn.gelu(widened, approximate=False).astype(jnp.bfloat16)
    )

    def unit_group(activated_block, narrow_block):
        partial = jnp.dot(activated_block, narrow_block, preferred_element_type=jnp.float32)
        return partial.astype(jnp.bfloat16).astype(jnp.float32)

    pair = unit_group(activated[:, :unit_count], narrow_weight) + unit_group(
        activated[:, unit_count:], partner_narrow
    )
    fed_total = reduce_tp(pair.astype(jnp.bfloat16), x_count, "x")
    updated = layer_norm(
        normed.astype(jnp.float32) + fed_total + narrow_bias.astype(jnp.float32),
        norm_gains[1],
        norm_biases[1],
    ).astype(jnp.bfloat16)
    returned = lax.all_to_all(
        updated.reshape(rows * tp_count, width // tp_count),
        ("req",) + TP,
        0,
        0,
        tiled=True,
    ).reshape(-1, tp_count, width // tp_count)
    hidden_out = returned.at[request_slot].get(mode="promise_in_bounds", unique_indices=True)
    return (hidden_out, new_cache)


def solution(mesh):
    req_count, tp_count = mesh.devices.shape
    split = Mesh(mesh.devices.reshape(req_count, tp_count // 2, 2), ("req",) + TP)
    in_specs = (
        P(None, "req", TP),
        P("req", None, TP),
        P("req", None, TP),
        P(),
        P(),
        P(),
        P(None, None, TP),
        P(None, TP),
        P(TP, None),
        P(),
        P(),
        P(),
        P(None, TP),
        P(TP),
        P(TP, None),
        P(),
    )
    out_specs = (P(None, "req", TP), P(None, "req", None, TP))
    return jax.shard_map(
        on_device, mesh=split, in_specs=in_specs, out_specs=out_specs, check_vma=False
    )
```

```python
import jax
import jax.numpy as jnp
from jax import lax
from jax.sharding import Mesh, PartitionSpec as P

HD = 64


def layer_norm(values, scale_row, shift_row):
    average = jnp.mean(values, axis=-1, keepdims=True)
    centred = values - average
    spread = jnp.mean(centred * centred, axis=-1, keepdims=True)
    return centred * lax.rsqrt(spread + 1e-05) * scale_row.astype(jnp.float32) + shift_row.astype(
        jnp.float32
    )


def split_heads(rows_block):
    return rows_block.reshape(rows_block.shape[0], -1, HD)


def block_scores(query_heads, keys_block, allowed):
    scores = jnp.einsum(
        "thd,shd->hts", query_heads, split_heads(keys_block), preferred_element_type=jnp.float32
    )
    return jnp.where(allowed[None], scores, -jnp.inf)


def to_rows(factor):
    return jnp.transpose(factor, (1, 0, 2))


def slot_attention(query_rows, key_rows, value_rows, slot_keys, slot_values, length, position):
    fresh_len = query_rows.shape[0]
    block_len = min(512, slot_keys.shape[0])
    block_count = slot_keys.shape[0] // block_len
    query_heads = split_heads(query_rows)
    self_mask = position[:, None] >= position[None, :]
    self_scores = block_scores(query_heads, key_rows, self_mask)
    row_top = jnp.max(self_scores, axis=2, keepdims=True)
    raised = jnp.exp(self_scores - row_top)
    row_total = jnp.sum(raised, axis=2, keepdims=True)
    context = jnp.einsum(
        "hts,shd->thd",
        raised.astype(jnp.bfloat16),
        split_heads(value_rows),
        preferred_element_type=jnp.float32,
    )
    positions = jnp.arange(block_len)

    def one_block(number, carry):
        old_top, old_total, running = carry
        begin_at = number * block_len
        keys_block = lax.dynamic_slice_in_dim(slot_keys, begin_at, block_len)
        values_block = lax.dynamic_slice_in_dim(slot_values, begin_at, block_len)
        allowed = jnp.broadcast_to((begin_at + positions < length)[None, :], (fresh_len, block_len))
        scores = block_scores(query_heads, keys_block, allowed)
        new_top = jnp.maximum(old_top, jnp.max(scores, axis=2, keepdims=True))
        factor = jnp.exp(old_top - new_top)
        block_raised = jnp.exp(scores - new_top)
        new_total = old_total * factor + jnp.sum(block_raised, axis=2, keepdims=True)
        added = jnp.einsum(
            "hts,shd->thd",
            block_raised.astype(jnp.bfloat16),
            split_heads(values_block),
            preferred_element_type=jnp.float32,
        )
        return (new_top, new_total, running * to_rows(factor) + added)

    row_top, row_total, context = lax.fori_loop(
        0, block_count, one_block, (row_top, row_total, context)
    )
    context = context / to_rows(row_total)
    return context.reshape(fresh_len, -1).astype(jnp.bfloat16)


TP = ("x", "core")


def gather_tp(block, tp_count, axis, names=TP):
    copies = jnp.broadcast_to(
        jnp.expand_dims(block, axis), block.shape[:axis] + (tp_count,) + block.shape[axis:]
    )
    got = lax.all_to_all(copies, names, axis, axis, tiled=True)
    return got.reshape(block.shape[:axis] + (-1,) + block.shape[axis + 1 :])


def reduce_tp(partial, tp_count, names=TP):
    rows = partial.shape[0] // tp_count
    got = lax.all_to_all(partial.reshape(tp_count, rows, -1), names, 0, 0, tiled=True)
    return jnp.sum(got.astype(jnp.float32), axis=0)


def from_partner(block):
    return lax.ppermute(block, "core", [(0, 1), (1, 0)])


def permute_rows(order, table):
    picks = (order[:, None] == jnp.arange(table.shape[0])[None, :]).astype(table.dtype)
    flat = table.reshape(table.shape[0], -1)
    moved = jnp.dot(picks, flat, preferred_element_type=jnp.float32).astype(table.dtype)
    return moved.reshape(table.shape)


def on_device(
    hidden_in,
    cache_keys,
    cache_values,
    cache_lengths,
    owner_order,
    request_slot,
    proj_weight,
    proj_bias,
    output_weight,
    output_bias,
    norm_gains,
    norm_biases,
    widen_weight,
    widen_bias,
    narrow_weight,
    narrow_bias,
):
    x_count = lax.axis_size("x")
    tp_count = x_count * lax.axis_size("core")
    tp_index = lax.axis_index(TP)
    partner_widen = from_partner(widen_weight)
    partner_widen_bias = from_partner(widen_bias)
    partner_narrow = from_partner(narrow_weight)
    partner_output = from_partner(output_weight)
    core_index = lax.axis_index("core")
    slot_index = lax.axis_index("req")
    length = cache_lengths[owner_order[slot_index]]
    routed_in = permute_rows(owner_order, hidden_in)
    chunk_len = routed_in.shape[1]
    own_cols = lax.all_to_all(
        jnp.transpose(routed_in, (1, 0, 2)), "req", split_axis=1, concat_axis=1, tiled=True
    )
    chunk_count = own_cols.shape[1]
    own_cols = own_cols.reshape(chunk_len * chunk_count, -1)
    fresh_len = own_cols.shape[0]
    width = own_cols.shape[1] * tp_count
    row_ids = jnp.arange(fresh_len)
    position = (row_ids % chunk_count) * chunk_len + row_ids // chunk_count
    token_rows = gather_tp(own_cols, tp_count, 1)
    projected = (
        jnp.einsum("td,cdf->ctf", token_rows, proj_weight, preferred_element_type=jnp.float32)
        + proj_bias.astype(jnp.float32)[:, None, :]
    )
    query_rows = (projected[0] * HD ** (-0.5)).astype(jnp.bfloat16)
    key_rows = projected[1].astype(jnp.bfloat16)
    value_rows = projected[2].astype(jnp.bfloat16)
    new_cache = jnp.stack([key_rows, value_rows], axis=0).reshape(2, chunk_len, chunk_count, -1)
    new_cache = jnp.transpose(new_cache, (0, 2, 1, 3)).reshape(2, 1, fresh_len, -1)
    context = slot_attention(
        query_rows, key_rows, value_rows, cache_keys[0], cache_values[0], length, position
    )
    rows = fresh_len // tp_count
    own_rows = lax.optimization_barrier(
        lax.dynamic_slice_in_dim(token_rows, tp_index * rows, rows).astype(jnp.float32)
        + output_bias.astype(jnp.float32)
    )
    halves = context.reshape(x_count, 2, rows, -1)
    kept = lax.dynamic_index_in_dim(halves, core_index, 1, keepdims=False)
    sent = lax.dynamic_index_in_dim(halves, 1 - core_index, 1, keepdims=False)
    got = from_partner(sent)

    def head_group(context_rows, weight_block):
        partial = jnp.dot(
            context_rows.reshape(x_count * rows, -1), weight_block, preferred_element_type=jnp.float32
        )
        return partial.astype(jnp.bfloat16).astype(jnp.float32)

    attended = reduce_tp(
        (head_group(kept, output_weight) + head_group(got, partner_output)).astype(jnp.bfloat16),
        x_count,
        "x",
    )
    pre_norm = own_rows + attended
    normed = layer_norm(pre_norm, norm_gains[0], norm_biases[0]).astype(jnp.bfloat16)
    average = jnp.mean(pre_norm, axis=-1, keepdims=True)
    centred = pre_norm - average
    spread = jnp.mean(centred * centred, axis=-1, keepdims=True)
    normed_copies = (
        jnp.broadcast_to(centred[None], (x_count,) + centred.shape)
        * lax.rsqrt(spread + 1e-05)
        * norm_gains[0].astype(jnp.float32)
        + norm_biases[0].astype(jnp.float32)
    ).astype(jnp.bfloat16)
    normed_half = lax.all_to_all(normed_copies, "x", 0, 0, tiled=True).reshape(-1, width)
    unit_count = widen_weight.shape[1]
    widened = jnp.dot(
        normed_half,
        jnp.concatenate([widen_weight, partner_widen], axis=1),
        preferred_element_type=jnp.float32,
    ) + jnp.concatenate([widen_bias, partner_widen_bias]).astype(jnp.float32)
    activated = lax.optimization_barrier(
        jax.nn.gelu(widened, approximate=False).astype(jnp.bfloat16)
    )

    def unit_group(activated_block, narrow_block):
        partial = jnp.dot(activated_block, narrow_block, preferred_element_type=jnp.float32)
        return partial.astype(jnp.bfloat16).astype(jnp.float32)

    pair = unit_group(activated[:, :unit_count], narrow_weight) + unit_group(
        activated[:, unit_count:], partner_narrow
    )
    fed_total = reduce_tp(pair.astype(jnp.bfloat16), x_count, "x")
    updated = layer_norm(
        normed.astype(jnp.float32) + fed_total + narrow_bias.astype(jnp.float32),
        norm_gains[1],
        norm_biases[1],
    ).astype(jnp.bfloat16)
    returned = lax.all_to_all(
        updated.reshape(rows * tp_count, width // tp_count),
        ("req",) + TP,
        0,
        0,
        tiled=True,
    ).reshape(-1, tp_count, width // tp_count)
    hidden_out = permute_rows(request_slot, returned)
    return (hidden_out, new_cache)


def solution(mesh):
    req_count, tp_count = mesh.devices.shape
    split = Mesh(mesh.devices.reshape(req_count, tp_count // 2, 2), ("req",) + TP)
    in_specs = (
        P(None, "req", TP),
        P("req", None, TP),
        P("req", None, TP),
        P(),
        P(),
        P(),
        P(None, None, TP),
        P(None, TP),
        P(TP, None),
        P(),
        P(),
        P(),
        P(None, TP),
        P(TP),
        P(TP, None),
        P(),
    )
    out_specs = (P(None, "req", TP), P(None, "req", None, TP))
    return jax.shard_map(
        on_device, mesh=split, in_specs=in_specs, out_specs=out_specs, check_vma=False
    )
```

```python
import jax
import jax.numpy as jnp
from jax import lax
from jax.sharding import Mesh, PartitionSpec as P

HD = 64


def layer_norm(values, scale_row, shift_row):
    average = jnp.mean(values, axis=-1, keepdims=True)
    centred = values - average
    spread = jnp.mean(centred * centred, axis=-1, keepdims=True)
    return centred * lax.rsqrt(spread + 1e-05) * scale_row.astype(jnp.float32) + shift_row.astype(
        jnp.float32
    )


def split_heads(rows_block):
    return rows_block.reshape(rows_block.shape[0], -1, HD)


def block_scores(query_heads, keys_block, allowed):
    scores = jnp.einsum(
        "thd,shd->hts", query_heads, split_heads(keys_block), preferred_element_type=jnp.float32
    )
    return jnp.where(allowed[None], scores, -jnp.inf)


def to_rows(factor):
    return jnp.transpose(factor, (1, 0, 2))


def slot_attention(query_rows, key_rows, value_rows, slot_keys, slot_values, length, position):
    fresh_len = query_rows.shape[0]
    block_len = min(512, slot_keys.shape[0])
    block_count = slot_keys.shape[0] // block_len
    query_heads = split_heads(query_rows)
    self_mask = position[:, None] >= position[None, :]
    self_scores = block_scores(query_heads, key_rows, self_mask)
    row_top = jnp.max(self_scores, axis=2, keepdims=True)
    raised = jnp.exp(self_scores - row_top)
    row_total = jnp.sum(raised, axis=2, keepdims=True)
    context = jnp.einsum(
        "hts,shd->thd",
        raised.astype(jnp.bfloat16),
        split_heads(value_rows),
        preferred_element_type=jnp.float32,
    )
    positions = jnp.arange(block_len)

    def one_block(number, carry):
        old_top, old_total, running = carry
        begin_at = number * block_len
        keys_block = lax.dynamic_slice_in_dim(slot_keys, begin_at, block_len)
        values_block = lax.dynamic_slice_in_dim(slot_values, begin_at, block_len)
        allowed = jnp.broadcast_to((begin_at + positions < length)[None, :], (fresh_len, block_len))
        scores = block_scores(query_heads, keys_block, allowed)
        new_top = jnp.maximum(old_top, jnp.max(scores, axis=2, keepdims=True))
        factor = jnp.exp(old_top - new_top)
        block_raised = jnp.exp(scores - new_top)
        new_total = old_total * factor + jnp.sum(block_raised, axis=2, keepdims=True)
        added = jnp.einsum(
            "hts,shd->thd",
            block_raised.astype(jnp.bfloat16),
            split_heads(values_block),
            preferred_element_type=jnp.float32,
        )
        return (new_top, new_total, running * to_rows(factor) + added)

    row_top, row_total, context = lax.fori_loop(
        0, block_count, one_block, (row_top, row_total, context)
    )
    context = context / to_rows(row_total)
    return context.reshape(fresh_len, -1).astype(jnp.bfloat16)


TP = ("x", "core")


def gather_tp(block, tp_count, axis, names=TP):
    copies = jnp.broadcast_to(
        jnp.expand_dims(block, axis), block.shape[:axis] + (tp_count,) + block.shape[axis:]
    )
    got = lax.all_to_all(copies, names, axis, axis, tiled=True)
    return got.reshape(block.shape[:axis] + (-1,) + block.shape[axis + 1 :])


def reduce_tp(partial, tp_count, names=TP):
    rows = partial.shape[0] // tp_count
    got = lax.all_to_all(partial.reshape(tp_count, rows, -1), names, 0, 0, tiled=True)
    return jnp.sum(got.astype(jnp.float32), axis=0)


def from_partner(block):
    return lax.ppermute(block, "core", [(0, 1), (1, 0)])


def permute_rows(order, table):
    picks = (order[:, None] == jnp.arange(table.shape[0])[None, :]).astype(table.dtype)
    flat = table.reshape(table.shape[0], -1)
    moved = jnp.dot(picks, flat, preferred_element_type=jnp.float32).astype(table.dtype)
    return moved.reshape(table.shape)


def on_device(
    hidden_in,
    cache_keys,
    cache_values,
    cache_lengths,
    owner_order,
    request_slot,
    proj_weight,
    proj_bias,
    output_weight,
    output_bias,
    norm_gains,
    norm_biases,
    widen_weight,
    widen_bias,
    narrow_weight,
    narrow_bias,
):
    x_count = lax.axis_size("x")
    tp_count = x_count * lax.axis_size("core")
    tp_index = lax.axis_index(TP)
    partner_widen = from_partner(widen_weight)
    partner_widen_bias = from_partner(widen_bias)
    partner_narrow = from_partner(narrow_weight)
    partner_output = from_partner(output_weight)
    core_index = lax.axis_index("core")
    slot_index = lax.axis_index("req")
    length = cache_lengths[owner_order[slot_index]]
    routed_in = permute_rows(owner_order, hidden_in)
    chunk_len = routed_in.shape[1]
    own_cols = lax.all_to_all(
        jnp.transpose(routed_in, (1, 0, 2)), "req", split_axis=1, concat_axis=1, tiled=True
    )
    chunk_count = own_cols.shape[1]
    own_cols = own_cols.reshape(chunk_len * chunk_count, -1)
    fresh_len = own_cols.shape[0]
    width = own_cols.shape[1] * tp_count
    row_ids = jnp.arange(fresh_len)
    position = (row_ids % chunk_count) * chunk_len + row_ids // chunk_count
    token_rows = gather_tp(own_cols, tp_count, 1)
    projected = (
        jnp.einsum("td,cdf->ctf", token_rows, proj_weight, preferred_element_type=jnp.float32)
        + proj_bias.astype(jnp.float32)[:, None, :]
    )
    query_rows = (projected[0] * HD ** (-0.5)).astype(jnp.bfloat16)
    key_rows = projected[1].astype(jnp.bfloat16)
    value_rows = projected[2].astype(jnp.bfloat16)
    new_cache = jnp.stack([key_rows, value_rows], axis=0).reshape(2, chunk_len, chunk_count, -1)
    new_cache = jnp.transpose(new_cache, (0, 2, 1, 3)).reshape(2, 1, fresh_len, -1)
    context = slot_attention(
        query_rows, key_rows, value_rows, cache_keys[0], cache_values[0], length, position
    )
    rows = fresh_len // tp_count
    own_rows = lax.optimization_barrier(
        lax.dynamic_slice_in_dim(token_rows, tp_index * rows, rows).astype(jnp.float32)
        + output_bias.astype(jnp.float32)
    )
    halves = context.reshape(x_count, 2, rows, -1)
    kept = lax.dynamic_index_in_dim(halves, core_index, 1, keepdims=False)
    sent = lax.dynamic_index_in_dim(halves, 1 - core_index, 1, keepdims=False)
    got = from_partner(sent)

    def head_group(context_rows, weight_block):
        partial = jnp.dot(
            context_rows.reshape(x_count * rows, -1), weight_block, preferred_element_type=jnp.float32
        )
        return partial.astype(jnp.bfloat16).astype(jnp.float32)

    attended = reduce_tp(
        (head_group(kept, output_weight) + head_group(got, partner_output)).astype(jnp.bfloat16),
        x_count,
        "x",
    )
    normed = layer_norm(
        own_rows + attended,
        norm_gains[0],
        norm_biases[0],
    ).astype(jnp.bfloat16)
    normed_half = gather_tp(normed, x_count, 0, "x")

    unit_count = widen_weight.shape[1]
    widened = jnp.dot(
        normed_half,
        jnp.concatenate([widen_weight, partner_widen], axis=1),
        preferred_element_type=jnp.float32,
    ) + jnp.concatenate([widen_bias, partner_widen_bias]).astype(jnp.float32)
    activated = lax.optimization_barrier(
        jax.nn.gelu(widened, approximate=False).astype(jnp.bfloat16)
    )

    def unit_group(activated_block, narrow_block):
        partial = jnp.dot(activated_block, narrow_block, preferred_element_type=jnp.float32)
        return partial.astype(jnp.bfloat16).astype(jnp.float32)

    pair = unit_group(activated[:, :unit_count], narrow_weight) + unit_group(
        activated[:, unit_count:], partner_narrow
    )
    fed_total = reduce_tp(pair.astype(jnp.bfloat16), x_count, "x")
    pieces = (rows, tp_count, width // tp_count)
    pre_out = (normed.astype(jnp.float32) + fed_total + narrow_bias.astype(jnp.float32)).reshape(pieces)
    average = jnp.mean(pre_out, axis=(1, 2), keepdims=True)
    centred = pre_out - average
    spread = jnp.mean(centred * centred, axis=(1, 2), keepdims=True)
    updated = (
        centred * lax.rsqrt(spread + 1e-05) * norm_gains[1].astype(jnp.float32).reshape(pieces[1:])
        + norm_biases[1].astype(jnp.float32).reshape(pieces[1:])
    ).astype(jnp.bfloat16)
    returned = lax.all_to_all(
        updated.reshape(rows * tp_count, width // tp_count),
        ("req",) + TP,
        0,
        0,
        tiled=True,
    ).reshape(-1, tp_count, width // tp_count)
    hidden_out = permute_rows(request_slot, returned)
    return (hidden_out, new_cache)


def solution(mesh):
    req_count, tp_count = mesh.devices.shape
    split = Mesh(mesh.devices.reshape(req_count, tp_count // 2, 2), ("req",) + TP)
    in_specs = (
        P(None, "req", TP),
        P("req", None, TP),
        P("req", None, TP),
        P(),
        P(),
        P(),
        P(None, None, TP),
        P(None, TP),
        P(TP, None),
        P(),
        P(),
        P(),
        P(None, TP),
        P(TP),
        P(TP, None),
        P(),
    )
    out_specs = (P(None, "req", TP), P(None, "req", None, TP))
    return jax.shard_map(
        on_device, mesh=split, in_specs=in_specs, out_specs=out_specs, check_vma=False
    )
```

```python
import jax
import jax.numpy as jnp
from jax import lax
from jax.sharding import Mesh, PartitionSpec as P

HD = 64


def layer_norm(values, scale_row, shift_row):
    average = jnp.mean(values, axis=-1, keepdims=True)
    centred = values - average
    spread = jnp.mean(centred * centred, axis=-1, keepdims=True)
    return centred * lax.rsqrt(spread + 1e-05) * scale_row.astype(jnp.float32) + shift_row.astype(
        jnp.float32
    )


def split_heads(rows_block):
    return rows_block.reshape(rows_block.shape[0], -1, HD)


def block_scores(query_heads, keys_block, allowed):
    scores = jnp.einsum(
        "thd,shd->hts", query_heads, split_heads(keys_block), preferred_element_type=jnp.float32
    )
    return jnp.where(allowed[None], scores, -jnp.inf)


def to_rows(factor):
    return jnp.transpose(factor, (1, 0, 2))


def slot_attention(query_rows, key_rows, value_rows, slot_keys, slot_values, length, position):
    fresh_len = query_rows.shape[0]
    block_len = min(512, slot_keys.shape[0])
    block_count = slot_keys.shape[0] // block_len
    query_heads = split_heads(query_rows)
    self_mask = position[:, None] >= position[None, :]
    self_scores = block_scores(query_heads, key_rows, self_mask)
    row_top = jnp.max(self_scores, axis=2, keepdims=True)
    raised = jnp.exp(self_scores - row_top)
    row_total = jnp.sum(raised, axis=2, keepdims=True)
    context = jnp.einsum(
        "hts,shd->thd",
        raised.astype(jnp.bfloat16),
        split_heads(value_rows),
        preferred_element_type=jnp.float32,
    )
    positions = jnp.arange(block_len)

    def one_block(number, carry):
        old_top, old_total, running = carry
        begin_at = number * block_len
        keys_block = lax.dynamic_slice_in_dim(slot_keys, begin_at, block_len)
        values_block = lax.dynamic_slice_in_dim(slot_values, begin_at, block_len)
        allowed = jnp.broadcast_to((begin_at + positions < length)[None, :], (fresh_len, block_len))
        scores = block_scores(query_heads, keys_block, allowed)
        new_top = jnp.maximum(old_top, jnp.max(scores, axis=2, keepdims=True))
        factor = jnp.exp(old_top - new_top)
        block_raised = jnp.exp(scores - new_top)
        new_total = old_total * factor + jnp.sum(block_raised, axis=2, keepdims=True)
        added = jnp.einsum(
            "hts,shd->thd",
            block_raised.astype(jnp.bfloat16),
            split_heads(values_block),
            preferred_element_type=jnp.float32,
        )
        return (new_top, new_total, running * to_rows(factor) + added)

    row_top, row_total, context = lax.fori_loop(
        0, block_count, one_block, (row_top, row_total, context)
    )
    context = context / to_rows(row_total)
    return context.reshape(fresh_len, -1).astype(jnp.bfloat16)


TP = ("x", "core")


def gather_tp(block, tp_count, axis, names=TP):
    copies = jnp.broadcast_to(
        jnp.expand_dims(block, axis), block.shape[:axis] + (tp_count,) + block.shape[axis:]
    )
    got = lax.all_to_all(copies, names, axis, axis, tiled=True)
    return got.reshape(block.shape[:axis] + (-1,) + block.shape[axis + 1 :])


def reduce_tp(partial, tp_count, names=TP):
    rows = partial.shape[0] // tp_count
    got = lax.all_to_all(partial.reshape(tp_count, rows, -1), names, 0, 0, tiled=True)
    return jnp.sum(got.astype(jnp.float32), axis=0)


def from_partner(block):
    return lax.ppermute(block, "core", [(0, 1), (1, 0)])


def permute_rows(order, table):
    picks = (order[:, None] == jnp.arange(table.shape[0])[None, :]).astype(table.dtype)
    flat = table.reshape(table.shape[0], -1)
    moved = jnp.dot(picks, flat, preferred_element_type=jnp.float32).astype(table.dtype)
    return moved.reshape(table.shape)


def on_device(
    hidden_in,
    cache_keys,
    cache_values,
    cache_lengths,
    owner_order,
    request_slot,
    proj_weight,
    proj_bias,
    output_weight,
    output_bias,
    norm_gains,
    norm_biases,
    widen_weight,
    widen_bias,
    narrow_weight,
    narrow_bias,
):
    x_count = lax.axis_size("x")
    tp_count = x_count * lax.axis_size("core")
    tp_index = lax.axis_index(TP)
    partner_widen = from_partner(widen_weight)
    partner_widen_bias = from_partner(widen_bias)
    partner_narrow = from_partner(narrow_weight)
    partner_output = from_partner(output_weight)
    core_index = lax.axis_index("core")
    slot_index = lax.axis_index("req")
    length = cache_lengths[owner_order[slot_index]]
    routed_in = permute_rows(owner_order, hidden_in)
    chunk_len = routed_in.shape[1]
    own_cols = lax.all_to_all(
        jnp.transpose(routed_in, (1, 0, 2)), "req", split_axis=1, concat_axis=1, tiled=True
    )
    chunk_count = own_cols.shape[1]
    own_cols = own_cols.reshape(chunk_len * chunk_count, -1)
    fresh_len = own_cols.shape[0]
    width = own_cols.shape[1] * tp_count
    row_ids = jnp.arange(fresh_len)
    position = (row_ids % chunk_count) * chunk_len + row_ids // chunk_count
    token_rows = gather_tp(own_cols, tp_count, 1)
    projected = (
        jnp.einsum("td,cdf->ctf", token_rows, proj_weight, preferred_element_type=jnp.float32)
        + proj_bias.astype(jnp.float32)[:, None, :]
    )
    query_rows = (projected[0] * HD ** (-0.5)).astype(jnp.bfloat16)
    key_rows = projected[1].astype(jnp.bfloat16)
    value_rows = projected[2].astype(jnp.bfloat16)
    new_cache = jnp.stack([key_rows, value_rows], axis=0).reshape(2, chunk_len, chunk_count, -1)
    new_cache = jnp.transpose(new_cache, (0, 2, 1, 3)).reshape(2, 1, fresh_len, -1)
    context = slot_attention(
        query_rows, key_rows, value_rows, cache_keys[0], cache_values[0], length, position
    )
    rows = fresh_len // tp_count
    own_rows = lax.optimization_barrier(
        lax.dynamic_slice_in_dim(token_rows, tp_index * rows, rows).astype(jnp.float32)
        + output_bias.astype(jnp.float32)
    )
    halves = context.reshape(x_count, 2, rows, -1)
    kept = lax.dynamic_index_in_dim(halves, core_index, 1, keepdims=False)
    sent = lax.dynamic_index_in_dim(halves, 1 - core_index, 1, keepdims=False)
    got = from_partner(sent)

    def head_group(context_rows, weight_block):
        partial = jnp.dot(
            context_rows.reshape(x_count * rows, -1), weight_block, preferred_element_type=jnp.float32
        )
        return partial.astype(jnp.bfloat16).astype(jnp.float32)

    attended = reduce_tp(
        (head_group(kept, output_weight) + head_group(got, partner_output)).astype(jnp.bfloat16),
        x_count,
        "x",
    )
    normed = layer_norm(
        own_rows + attended,
        norm_gains[0],
        norm_biases[0],
    ).astype(jnp.bfloat16)
    normed_half = gather_tp(normed, x_count, 0, "x")

    unit_count = widen_weight.shape[1]
    widened = jnp.dot(
        normed_half,
        jnp.concatenate([widen_weight, partner_widen], axis=1),
        preferred_element_type=jnp.float32,
    ) + jnp.concatenate([widen_bias, partner_widen_bias]).astype(jnp.float32)
    activated = lax.optimization_barrier(
        jax.nn.gelu(widened, approximate=False).astype(jnp.bfloat16)
    )

    def unit_group(activated_block, narrow_block):
        partial = jnp.dot(activated_block, narrow_block, preferred_element_type=jnp.float32)
        return partial.astype(jnp.bfloat16).astype(jnp.float32)

    pair = unit_group(activated[:, :unit_count], narrow_weight) + unit_group(
        activated[:, unit_count:], partner_narrow
    )
    fed_total = reduce_tp(pair.astype(jnp.bfloat16), x_count, "x")
    updated = layer_norm(
        normed.astype(jnp.float32) + fed_total + narrow_bias.astype(jnp.float32),
        norm_gains[1],
        norm_biases[1],
    ).astype(jnp.bfloat16)
    returned = lax.all_to_all(
        updated.reshape(rows * tp_count, width // tp_count),
        ("req",) + TP,
        0,
        0,
        tiled=True,
    ).reshape(-1, tp_count, width // tp_count)
    hidden_out = returned.at[request_slot].get(mode="promise_in_bounds", unique_indices=True)
    return (hidden_out, new_cache)


def solution(mesh):
    req_count, tp_count = mesh.devices.shape
    split = Mesh(mesh.devices.reshape(req_count, tp_count // 2, 2), ("req",) + TP)
    in_specs = (
        P(None, "req", TP),
        P("req", None, TP),
        P("req", None, TP),
        P(),
        P(),
        P(),
        P(None, None, TP),
        P(None, TP),
        P(TP, None),
        P(),
        P(),
        P(),
        P(None, TP),
        P(TP),
        P(TP, None),
        P(),
    )
    out_specs = (P(None, "req", TP), P(None, "req", None, TP))
    return jax.shard_map(
        on_device, mesh=split, in_specs=in_specs, out_specs=out_specs, check_vma=False
    )
```
